32 devices in a mesh: dp: 4 (over x, core), tensor: 8 (over z, y).
Axes of the slice: x: 2, y: 2, z: 4, core: 2. Of those that a mesh axis runs over, the one named last changes fastest.
Arguments:
- grad: bfloat16 [4, 576, 6144], P('dp', 'tensor'), as said below
- momentum: float32 [4, 576, 6144], P('dp', 'tensor'), may hold values from -6 to 6
- owner: int32 [4], replicated, may hold values from 0 to 3, each once
Outputs:
- update: bfloat16 [4, 576, 6144], P(None, 'tensor')
- new_momentum: float32 [4, 576, 6144], P('dp', 'tensor')
The draws below stay inside these ranges and needn't reach their ends.
Inputs may be any that keep to these rules, and one draw needn't show every extreme that they name: owner names each matrix 0 to 3 exactly once. `grad`: gradient entries are finite; every matrix has full rank.
All inputs are finite; a program needn't handle non-finite values.
Results may differ from the reference program's by a relative error of at most 0.0013.
The reference program's roundings to bfloat16 on the way (of `iterate`, `gram`, `poly` and `scaled`) count: a program that leaves them out, or rounds other values in their place, can miss the bound.
Values may be sent and summed in bfloat16 or wider, within the bound.
No kernel may reach another device: no remote copies, remote signals or barrier semaphores. Data moves between devices by JAX's collectives and lax.ppermute only.
A program may use at most 64 MiB of HBM per device.

```python
import math
import jax
import jax.numpy as jnp
from jax import lax

M = 576
N = 6144
ITERS = 2
MATS = 4
N_TENSOR = 8


def draw_grad(key, part):
    key_rows = jax.random.fold_in(key, 11)
    key_cols = jax.random.fold_in(key, 12)
    key_base = jax.random.fold_in(key, 13)
    key_blocks = jax.random.fold_in(key, 15)
    position = jnp.arange(M, dtype=jnp.float32) / M
    rise = jnp.exp(math.log(3.0) * position)[None, :, None]
    row_scale = rise * jnp.exp(math.log(10.0) * jax.random.uniform(key_rows, (MATS, M, 1), jnp.float32))
    col_scale = jnp.exp(math.log(10.0) * jax.random.uniform(key_cols, (MATS, 1, N), jnp.float32))
    block_draw = jnp.exp(math.log(20.0) * jax.random.uniform(key_blocks, (MATS, N_TENSOR), jnp.float32))
    block_index = jnp.arange(N, dtype=jnp.int32) // (N // N_TENSOR)
    block_scale = jnp.take(block_draw, block_index, axis=1)[:, None, :]
    base = jax.random.normal(key_base, (MATS, M, N), jnp.float32)
    return (0.04 * base * row_scale * col_scale * block_scale).astype(jnp.bfloat16)


def block_levels(key, dims, shards, smallest, top_value):
    def one(dim, parts):
        heights = jax.random.uniform(jax.random.fold_in(jax.random.fold_in(key, 6), dim), (parts,), jnp.float32, smallest / len(shards), top_value / len(shards))
        return jnp.repeat(jnp.exp(heights), dims[dim] // parts).reshape((-1,) + (1,) * (len(dims) - dim - 1))

    level = one(*shards[0])
    for cut in shards[1:]:
        level = level * one(*cut)
    return level


def noise(stream_key, extent, scale, reach, pieces=(), kind=jnp.bfloat16):
    entries = jax.random.normal(stream_key, extent, jnp.float32) * scale
    if len(pieces) > 0:
        entries = block_levels(stream_key, extent, pieces, -0.22, 0.18) * entries
    return jnp.clip(entries, min=-reach, max=reach).astype(kind)


def setup_inputs(seed: int = 0) -> dict:
    splits = jax.random.split(jax.random.key(seed), 4)
    return {
        "grad": draw_grad(jax.random.fold_in(splits[3], 71), 0),
        "momentum": noise(splits[1], (MATS, M, N), 1.0, 6.0, ((0, 4), (1, 8)), jnp.float32),
        "owner": jax.random.permutation(splits[2], MATS).astype(jnp.int32),
    }


coef_a = 3.4445
coef_b = -4.775
coef_c = 2.0315
decay = 0.95
eps = 1e-07

def orthogonalize(start):
    current = start
    for step in range(ITERS):
        gram = jnp.dot(current, current.T, preferred_element_type=jnp.float32).astype(jnp.bfloat16)
        square = jnp.dot(gram, gram, preferred_element_type=jnp.float32)
        poly = (coef_b * gram.astype(jnp.float32) + coef_c * square).astype(jnp.bfloat16)
        current = (coef_a * current.astype(jnp.float32) + jnp.dot(poly, current, preferred_element_type=jnp.float32)).astype(jnp.bfloat16)
    return current

def reference(grad, momentum, owner):
    new_momentum = decay * momentum + grad.astype(jnp.float32)
    direction = grad.astype(jnp.float32) + decay * new_momentum
    total = lax.optimization_barrier(jnp.sum(direction * direction, axis=(1, 2), keepdims=True))
    iterate = (direction / (jnp.sqrt(total) + eps)).astype(jnp.bfloat16)
    final = lax.map(orthogonalize, iterate)
    factor = 0.2 * math.sqrt(max(M, N))
    scaled = (factor * final.astype(jnp.float32)).astype(jnp.bfloat16)
    order = jnp.argsort(owner).astype(jnp.int32)
    update = jnp.take(scaled, order, axis=0)
    return (update, new_momentum)
```

```python
import math

import jax
import jax.numpy as jnp
from jax import lax
from jax.sharding import PartitionSpec as P

M = 576
N = 6144
ITERS = 2


coef_a = 3.4445
coef_b = -4.775
coef_c = 2.0315
decay = 0.95
eps = 1e-07


def _shift_pairs(size, s):
    return [(i, (i + s) % size) for i in range(size)]


def total_over(value, axis, size):
    if size & (size - 1) == 0:
        bit = 1
        while bit < size:
            value = value + lax.ppermute(value, axis, [(i, i ^ bit) for i in range(size)])
            bit *= 2
        return value
    return lax.psum(value, axis)


def gram_allreduce(partial, axis, size):
    n = partial.shape[0]
    h = n // 2
    upper_a = partial[:h, :h]
    block_b = partial[:h, h:]
    lower_c = partial[h:, h:]
    row = lax.broadcasted_iota(jnp.int32, (h, h), 0)
    col = lax.broadcasted_iota(jnp.int32, (h, h), 1)
    folded = jnp.where(row <= col, upper_a, lower_c)
    diag_c = jnp.diagonal(lower_c)
    payload = jnp.concatenate([folded, block_b], axis=1)
    extra = jnp.concatenate([diag_c, jnp.zeros((h,), jnp.float32)])[None, :]
    rows = -(-(h + 1) // size) * size
    payload = jnp.concatenate(
        [payload, extra, jnp.zeros((rows - h - 1, 2 * h), jnp.float32)], axis=0
    )
    per = rows // size
    blocks = payload.reshape(size, per, 2 * h)
    me = lax.axis_index(axis)
    order = (me + jnp.arange(size, dtype=jnp.int32)) % size
    rolled = jnp.take(blocks, order, axis=0)
    acc = rolled[0]
    for s in range(1, size):
        acc = acc + lax.ppermute(rolled[s], axis, _shift_pairs(size, s))
    mine = acc.astype(jnp.bfloat16)
    got = [mine] + [
        lax.ppermute(mine, axis, _shift_pairs(size, s)) for s in range(1, size)
    ]
    stacked = jnp.stack(got)
    back = (me - jnp.arange(size, dtype=jnp.int32)) % size
    full = jnp.take(stacked, back, axis=0).reshape(rows, 2 * h)
    folded_r = full[:h, :h]
    block_br = full[:h, h:]
    diag_cr = full[h, :h]
    upper_r = jnp.where(row <= col, folded_r, folded_r.T)
    lower_r = jnp.where(row > col, folded_r, folded_r.T)
    lower_r = jnp.where(row == col, diag_cr[None, :], lower_r)
    top = jnp.concatenate([upper_r, block_br], axis=1)
    bottom = jnp.concatenate([block_br.T, lower_r], axis=1)
    return jnp.concatenate([top, bottom], axis=0)


def per_device(grad, momentum, owner):
    size = lax.axis_size("tensor")
    new_momentum = decay * momentum + grad.astype(jnp.float32)
    direction = grad.astype(jnp.float32) + decay * new_momentum
    total = total_over(jnp.sum(direction * direction), "tensor", size)
    rows_here = (direction[0] / (jnp.sqrt(total) + eps)).astype(jnp.bfloat16)
    columns = lax.all_to_all(rows_here, "tensor", split_axis=1, concat_axis=0, tiled=True)
    for step in range(ITERS):
        partial = jnp.dot(columns, columns.T, preferred_element_type=jnp.float32)
        gram = gram_allreduce(partial, "tensor", size)
        square = jnp.dot(gram, gram, preferred_element_type=jnp.float32)
        poly = (coef_b * gram.astype(jnp.float32) + coef_c * square).astype(jnp.bfloat16)
        applied = jnp.dot(poly, columns, preferred_element_type=jnp.float32)
        columns = (coef_a * columns.astype(jnp.float32) + applied).astype(jnp.bfloat16)
    factor = 0.2 * math.sqrt(max(M, N))
    back_rows = lax.all_to_all(columns, "tensor", split_axis=0, concat_axis=1, tiled=True)
    scaled = (factor * back_rows.astype(jnp.float32)).astype(jnp.bfloat16)
    every_slot = lax.all_gather(scaled[None], "dp", axis=0, tiled=True)
    slots = every_slot.shape[0]
    ids = jnp.arange(slots, dtype=jnp.int32)
    inverse = jnp.sum(
        jnp.where(owner[None, :] == ids[:, None], ids[None, :], 0), axis=1
    )
    update = jnp.take(every_slot, inverse, axis=0)
    return (update, new_momentum)


def solution(mesh):
    in_specs = (P("dp", "tensor", None), P("dp", "tensor", None), P())
    out_specs = (P(None, "tensor", None), P("dp", "tensor", None))
    return jax.shard_map(
        per_device, mesh=mesh, in_specs=in_specs, out_specs=out_specs, check_vma=False
    )
```

```python
import math

import jax
import jax.numpy as jnp
from jax import lax
from jax.sharding import PartitionSpec as P

M = 576
N = 6144
ITERS = 2


coef_a = 3.4445
coef_b = -4.775
coef_c = 2.0315
decay = 0.95
eps = 1e-07


def _shift_pairs(size, s):
    return [(i, (i + s) % size) for i in range(size)]


def total_over(value, axis, size):
    if size & (size - 1) == 0:
        bit = 1
        while bit < size:
            value = value + lax.ppermute(value, axis, [(i, i ^ bit) for i in range(size)])
            bit *= 2
        return value
    return lax.psum(value, axis)


def gram_allreduce(partial, axis, size):
    n = partial.shape[0]
    h = n // 2
    upper_a = partial[:h, :h]
    block_b = partial[:h, h:]
    lower_c = partial[h:, h:]
    row = lax.broadcasted_iota(jnp.int32, (h, h), 0)
    col = lax.broadcasted_iota(jnp.int32, (h, h), 1)
    folded = jnp.where(row <= col, upper_a, lower_c)
    diag_c = jnp.diagonal(lower_c)
    payload = jnp.concatenate([folded, block_b], axis=1)
    extra = jnp.concatenate([diag_c, jnp.zeros((h,), jnp.float32)])[None, :]
    rows = -(-(h + 1) // size) * size
    payload = jnp.concatenate(
        [payload, extra, jnp.zeros((rows - h - 1, 2 * h), jnp.float32)], axis=0
    )
    per = rows // size
    blocks = payload.reshape(size, per, 2 * h)
    me = lax.axis_index(axis)
    order = (me + jnp.arange(size, dtype=jnp.int32)) % size
    rolled = jnp.take(blocks, order, axis=0)
    acc = rolled[0]
    for s in range(1, size):
        acc = acc + lax.ppermute(rolled[s], axis, _shift_pairs(size, s))
    mine = acc.astype(jnp.bfloat16)
    got = [mine] + [
        lax.ppermute(mine, axis, _shift_pairs(size, s)) for s in range(1, size)
    ]
    stacked = jnp.stack(got)
    back = (me - jnp.arange(size, dtype=jnp.int32)) % size
    full = jnp.take(stacked, back, axis=0).reshape(rows, 2 * h)
    folded_r = full[:h, :h]
    block_br = full[:h, h:]
    diag_cr = full[h, :h]
    upper_r = jnp.where(row <= col, folded_r, folded_r.T)
    lower_r = jnp.where(row > col, folded_r, folded_r.T)
    lower_r = jnp.where(row == col, diag_cr[None, :], lower_r)
    top = jnp.concatenate([upper_r, block_br], axis=1)
    bottom = jnp.concatenate([block_br.T, lower_r], axis=1)
    return jnp.concatenate([top, bottom], axis=0)


def per_device(grad, momentum, owner):
    size = lax.axis_size("tensor")
    new_momentum = decay * momentum + grad.astype(jnp.float32)
    direction = grad.astype(jnp.float32) + decay * new_momentum
    total = total_over(jnp.sum(direction * direction), "tensor", size)
    rows_here = (direction[0] / (jnp.sqrt(total) + eps)).astype(jnp.bfloat16)
    columns = lax.all_to_all(rows_here, "tensor", split_axis=1, concat_axis=0, tiled=True)
    for step in range(ITERS):
        partial = jnp.dot(columns, columns.T, preferred_element_type=jnp.float32)
        gram = gram_allreduce(partial, "tensor", size)
        square = jnp.dot(gram, gram, preferred_element_type=jnp.float32)
        poly = (coef_b * gram.astype(jnp.float32) + coef_c * square).astype(jnp.bfloat16)
        applied = jnp.dot(poly, columns, preferred_element_type=jnp.float32)
        columns = (coef_a * columns.astype(jnp.float32) + applied).astype(jnp.bfloat16)
    factor = 0.2 * math.sqrt(max(M, N))
    per = columns.shape[0] // size
    half = per // 2
    blocks = columns.reshape(size, per, columns.shape[1])
    gathered = []
    for lo, hi in ((0, half), (half, per)):
        piece = blocks[:, lo:hi, :].reshape(size * (hi - lo), columns.shape[1])
        back_rows = lax.all_to_all(piece, "tensor", split_axis=0, concat_axis=1, tiled=True)
        scaled = (factor * back_rows.astype(jnp.float32)).astype(jnp.bfloat16)
        gathered.append(lax.all_gather(scaled[None], "dp", axis=0, tiled=True))
    every_slot = jnp.concatenate(gathered, axis=1)
    slots = every_slot.shape[0]
    ids = jnp.arange(slots, dtype=jnp.int32)
    inverse = jnp.sum(
        jnp.where(owner[None, :] == ids[:, None], ids[None, :], 0), axis=1
    )
    update = jnp.take(every_slot, inverse, axis=0)
    return (update, new_momentum)


def solution(mesh):
    in_specs = (P("dp", "tensor", None), P("dp", "tensor", None), P())
    out_specs = (P(None, "tensor", None), P("dp", "tensor", None))
    return jax.shard_map(
        per_device, mesh=mesh, in_specs=in_specs, out_specs=out_specs, check_vma=False
    )
```

```python
import math

import jax
import jax.numpy as jnp
from jax import lax
from jax.sharding import PartitionSpec as P

M = 576
N = 6144
ITERS = 2


coef_a = 3.4445
coef_b = -4.775
coef_c = 2.0315
decay = 0.95
eps = 1e-07


def _shift_pairs(size, s):
    return [(i, (i + s) % size) for i in range(size)]


def total_over(value, axis, size):
    if size & (size - 1) == 0:
        bit = 1
        while bit < size:
            value = value + lax.ppermute(value, axis, [(i, i ^ bit) for i in range(size)])
            bit *= 2
        return value
    return lax.psum(value, axis)


def gram_allreduce(partial, axis, size):
    n = partial.shape[0]
    h = n // 2
    upper_a = partial[:h, :h]
    block_b = partial[:h, h:]
    lower_c = partial[h:, h:]
    row = lax.broadcasted_iota(jnp.int32, (h, h), 0)
    col = lax.broadcasted_iota(jnp.int32, (h, h), 1)
    folded = jnp.where(row <= col, upper_a, lower_c)
    diag_c = jnp.diagonal(lower_c)
    payload = jnp.concatenate([folded, block_b], axis=1)
    extra = jnp.concatenate([diag_c, jnp.zeros((h,), jnp.float32)])[None, :]
    rows = -(-(h + 1) // size) * size
    payload = jnp.concatenate(
        [payload, extra, jnp.zeros((rows - h - 1, 2 * h), jnp.float32)], axis=0
    )
    per = rows // size
    blocks = payload.reshape(size, per, 2 * h)
    me = lax.axis_index(axis)
    order = (me + jnp.arange(size, dtype=jnp.int32)) % size
    rolled = jnp.take(blocks, order, axis=0)
    acc = rolled[0]
    for s in range(1, size):
        acc = acc + lax.ppermute(rolled[s], axis, _shift_pairs(size, s))
    mine = acc.astype(jnp.bfloat16)
    got = [mine] + [
        lax.ppermute(mine, axis, _shift_pairs(size, s)) for s in range(1, size)
    ]
    stacked = jnp.stack(got)
    back = (me - jnp.arange(size, dtype=jnp.int32)) % size
    full = jnp.take(stacked, back, axis=0).reshape(rows, 2 * h)
    folded_r = full[:h, :h]
    block_br = full[:h, h:]
    diag_cr = full[h, :h]
    upper_r = jnp.where(row <= col, folded_r, folded_r.T)
    lower_r = jnp.where(row > col, folded_r, folded_r.T)
    lower_r = jnp.where(row == col, diag_cr[None, :], lower_r)
    top = jnp.concatenate([upper_r, block_br], axis=1)
    bottom = jnp.concatenate([block_br.T, lower_r], axis=1)
    return jnp.concatenate([top, bottom], axis=0)


def gather_slots(mine, axis, size):
    if size & (size - 1) != 0:
        full = lax.all_gather(mine[None], axis, axis=0, tiled=True)
        me = lax.axis_index(axis)
        return jnp.take(full, jnp.arange(size, dtype=jnp.int32) ^ me, axis=0, mode="clip")
    held = {0: mine}
    bit = size // 2
    while bit >= 1:
        keys = sorted(held)
        sent = jnp.stack([held[j] for j in keys])
        got = lax.ppermute(sent, axis, [(i, i ^ bit) for i in range(size)])
        for n, j in enumerate(keys):
            held[j ^ bit] = got[n]
        bit //= 2
    return jnp.stack([held[j] for j in range(size)])


def per_device(grad, momentum, owner):
    size = lax.axis_size("tensor")
    new_momentum = decay * momentum + grad.astype(jnp.float32)
    direction = grad.astype(jnp.float32) + decay * new_momentum
    total = total_over(jnp.sum(direction * direction), "tensor", size)
    rows_here = (direction[0] / (jnp.sqrt(total) + eps)).astype(jnp.bfloat16)
    columns = lax.all_to_all(rows_here, "tensor", split_axis=1, concat_axis=0, tiled=True)
    for step in range(ITERS):
        partial = jnp.dot(columns, columns.T, preferred_element_type=jnp.float32)
        gram = gram_allreduce(partial, "tensor", size)
        square = jnp.dot(gram, gram, preferred_element_type=jnp.float32)
        poly = (coef_b * gram.astype(jnp.float32) + coef_c * square).astype(jnp.bfloat16)
        applied = jnp.dot(poly, columns, preferred_element_type=jnp.float32)
        columns = (coef_a * columns.astype(jnp.float32) + applied).astype(jnp.bfloat16)
    factor = 0.2 * math.sqrt(max(M, N))
    per = columns.shape[0] // size
    half = per // 2
    blocks = columns.reshape(size, per, columns.shape[1])
    slots = lax.axis_size("dp")
    ids = jnp.arange(slots, dtype=jnp.int32)
    inverse = jnp.sum(
        jnp.where(owner[None, :] == ids[:, None], ids[None, :], 0), axis=1
    )
    where_from = inverse ^ lax.axis_index("dp")
    pieces = []
    for lo, hi in ((0, half), (half, per)):
        piece = blocks[:, lo:hi, :].reshape(size * (hi - lo), columns.shape[1])
        back_rows = lax.all_to_all(piece, "tensor", split_axis=0, concat_axis=1, tiled=True)
        scaled = (factor * back_rows.astype(jnp.float32)).astype(jnp.bfloat16)
        held = gather_slots(scaled, "dp", slots)
        pieces.append(held)
    rows = []
    for m in range(slots):
        rows.append(
            jnp.concatenate(
                [lax.dynamic_index_in_dim(p, where_from[m], 0, keepdims=True) for p in pieces],
                axis=1,
            )
        )
    update = jnp.concatenate(rows, axis=0)
    return (update, new_momentum)


def solution(mesh):
    in_specs = (P("dp", "tensor", None), P("dp", "tensor", None), P())
    out_specs = (P(None, "tensor", None), P("dp", "tensor", None))
    return jax.shard_map(
        per_device, mesh=mesh, in_specs=in_specs, out_specs=out_specs, check_vma=False
    )
```

```python
import math

import jax
import jax.numpy as jnp
from jax import lax
from jax.sharding import PartitionSpec as P

M = 576
N = 6144
ITERS = 2


coef_a = 3.4445
coef_b = -4.775
coef_c = 2.0315
decay = 0.95
eps = 1e-07


def _shift_pairs(size, s):
    return [(i, (i + s) % size) for i in range(size)]


def total_over(value, axis, size):
    spread = jnp.broadcast_to(value, (size, 1))
    got = lax.all_to_all(spread, axis, split_axis=0, concat_axis=0, tiled=True)
    return jnp.sum(got)


def gram_allreduce(partial, axis, size):
    n = partial.shape[0]
    h = n // 2
    upper_a = partial[:h, :h]
    block_b = partial[:h, h:]
    lower_c = partial[h:, h:]
    row = lax.broadcasted_iota(jnp.int32, (h, h), 0)
    col = lax.broadcasted_iota(jnp.int32, (h, h), 1)
    folded = jnp.where(row <= col, upper_a, lower_c)
    diag_c = jnp.diagonal(lower_c)
    payload = jnp.concatenate([folded, block_b], axis=1)
    extra = jnp.concatenate([diag_c, jnp.zeros((h,), jnp.float32)])[None, :]
    rows = -(-(h + 1) // size) * size
    payload = jnp.concatenate(
        [payload, extra, jnp.zeros((rows - h - 1, 2 * h), jnp.float32)], axis=0
    )
    per = rows // size
    blocks = payload.reshape(size, per, 2 * h)
    me = lax.axis_index(axis)
    order = (me + jnp.arange(size, dtype=jnp.int32)) % size
    rolled = jnp.take(blocks, order, axis=0)
    acc = rolled[0]
    for s in range(1, size):
        acc = acc + lax.ppermute(rolled[s], axis, _shift_pairs(size, s))
    mine = acc.astype(jnp.bfloat16)
    spread = jnp.broadcast_to(mine[None], (size,) + mine.shape)
    full = lax.all_to_all(spread, axis, split_axis=0, concat_axis=0, tiled=True).reshape(rows, 2 * h)
    folded_r = full[:h, :h]
    block_br = full[:h, h:]
    diag_cr = full[h, :h]
    upper_r = jnp.where(row <= col, folded_r, folded_r.T)
    lower_r = jnp.where(row > col, folded_r, folded_r.T)
    lower_r = jnp.where(row == col, diag_cr[None, :], lower_r)
    top = jnp.concatenate([upper_r, block_br], axis=1)
    bottom = jnp.concatenate([block_br.T, lower_r], axis=1)
    return jnp.concatenate([top, bottom], axis=0)


def gather_slots(mine, axis, size):
    if size & (size - 1) != 0:
        full = lax.all_gather(mine[None], axis, axis=0, tiled=True)
        me = lax.axis_index(axis)
        return jnp.take(full, jnp.arange(size, dtype=jnp.int32) ^ me, axis=0, mode="clip")
    held = {0: mine}
    bit = size // 2
    while bit >= 1:
        keys = sorted(held)
        sent = jnp.stack([held[j] for j in keys])
        got = lax.ppermute(sent, axis, [(i, i ^ bit) for i in range(size)])
        for n, j in enumerate(keys):
            held[j ^ bit] = got[n]
        bit //= 2
    return jnp.stack([held[j] for j in range(size)])


def per_device(grad, momentum, owner):
    size = lax.axis_size("tensor")
    new_momentum = decay * momentum + grad.astype(jnp.float32)
    direction = grad.astype(jnp.float32) + decay * new_momentum
    total = total_over(jnp.sum(direction * direction), "tensor", size)
    rows_here = (direction[0] / (jnp.sqrt(total) + eps)).astype(jnp.bfloat16)
    columns = lax.all_to_all(rows_here, "tensor", split_axis=1, concat_axis=0, tiled=True)
    for step in range(ITERS):
        partial = jnp.dot(columns, columns.T, preferred_element_type=jnp.float32)
        gram = gram_allreduce(partial, "tensor", size)
        square = jnp.dot(gram, gram, preferred_element_type=jnp.float32)
        poly = (coef_b * gram.astype(jnp.float32) + coef_c * square).astype(jnp.bfloat16)
        applied = jnp.dot(poly, columns, preferred_element_type=jnp.float32)
        columns = (coef_a * columns.astype(jnp.float32) + applied).astype(jnp.bfloat16)
    factor = 0.2 * math.sqrt(max(M, N))
    per = columns.shape[0] // size
    half = per // 2
    blocks = columns.reshape(size, per, columns.shape[1])
    slots = lax.axis_size("dp")
    ids = jnp.arange(slots, dtype=jnp.int32)
    inverse = jnp.sum(
        jnp.where(owner[None, :] == ids[:, None], ids[None, :], 0), axis=1
    )
    where_from = inverse ^ lax.axis_index("dp")
    pieces = []
    for lo, hi in ((0, half), (half, per)):
        piece = blocks[:, lo:hi, :].reshape(size * (hi - lo), columns.shape[1])
        back_rows = lax.all_to_all(piece, "tensor", split_axis=0, concat_axis=1, tiled=True)
        scaled = (factor * back_rows.astype(jnp.float32)).astype(jnp.bfloat16)
        held = gather_slots(scaled, "dp", slots)
        pieces.append(held)
    rows = []
    for m in range(slots):
        rows.append(
            jnp.concatenate(
                [lax.dynamic_index_in_dim(p, where_from[m], 0, keepdims=True) for p in pieces],
                axis=1,
            )
        )
    update = jnp.concatenate(rows, axis=0)
    return (update, new_momentum)


def solution(mesh):
    in_specs = (P("dp", "tensor", None), P("dp", "tensor", None), P())
    out_specs = (P(None, "tensor", None), P("dp", "tensor", None))
    return jax.shard_map(
        per_device, mesh=mesh, in_specs=in_specs, out_specs=out_specs, check_vma=False
    )
```

```python
import math

import jax
import jax.numpy as jnp
from jax import lax
from jax.sharding import PartitionSpec as P

M = 576
N = 6144
ITERS = 2


coef_a = 3.4445
coef_b = -4.775
coef_c = 2.0315
decay = 0.95
eps = 1e-07


def _shift_pairs(size, s):
    return [(i, (i + s) % size) for i in range(size)]


def total_over(value, axis, size):
    spread = jnp.broadcast_to(value, (size, 1))
    got = lax.all_to_all(spread, axis, split_axis=0, concat_axis=0, tiled=True)
    return jnp.sum(got)


def gram_allreduce(partial, axis, size):
    n = partial.shape[0]
    h = n // 2
    upper_a = partial[:h, :h]
    block_b = partial[:h, h:]
    lower_c = partial[h:, h:]
    row = lax.broadcasted_iota(jnp.int32, (h, h), 0)
    col = lax.broadcasted_iota(jnp.int32, (h, h), 1)
    folded = jnp.where(row <= col, upper_a, lower_c)
    diag_c = jnp.diagonal(lower_c)
    payload = jnp.concatenate([folded, block_b], axis=1)
    extra = jnp.concatenate([diag_c, jnp.zeros((h,), jnp.float32)])[None, :]
    rows = -(-(h + 1) // size) * size
    payload = jnp.concatenate(
        [payload, extra, jnp.zeros((rows - h - 1, 2 * h), jnp.float32)], axis=0
    )
    per = rows // size
    blocks = payload.reshape(size, per, 2 * h)
    me = lax.axis_index(axis)
    acc = lax.dynamic_index_in_dim(blocks, me, 0, keepdims=False)
    for s in range(1, size):
        outgoing = lax.dynamic_index_in_dim(blocks, (me + s) % size, 0, keepdims=False)
        acc = acc + lax.ppermute(outgoing, axis, _shift_pairs(size, s))
    mine = acc.astype(jnp.bfloat16)
    spread = jnp.broadcast_to(mine[None], (size,) + mine.shape)
    full = lax.all_to_all(spread, axis, split_axis=0, concat_axis=0, tiled=True).reshape(rows, 2 * h)
    folded_r = full[:h, :h]
    block_br = full[:h, h:]
    diag_cr = full[h, :h]
    upper_r = jnp.where(row <= col, folded_r, folded_r.T)
    lower_r = jnp.where(row > col, folded_r, folded_r.T)
    lower_r = jnp.where(row == col, diag_cr[None, :], lower_r)
    top = jnp.concatenate([upper_r, block_br], axis=1)
    bottom = jnp.concatenate([block_br.T, lower_r], axis=1)
    return jnp.concatenate([top, bottom], axis=0)


def gather_slots(mine, axis, size):
    if size & (size - 1) != 0:
        full = lax.all_gather(mine[None], axis, axis=0, tiled=True)
        me = lax.axis_index(axis)
        return jnp.take(full, jnp.arange(size, dtype=jnp.int32) ^ me, axis=0, mode="clip")
    held = {0: mine}
    bit = size // 2
    while bit >= 1:
        keys = sorted(held)
        sent = jnp.stack([held[j] for j in keys])
        got = lax.ppermute(sent, axis, [(i, i ^ bit) for i in range(size)])
        for n, j in enumerate(keys):
            held[j ^ bit] = got[n]
        bit //= 2
    return jnp.stack([held[j] for j in range(size)])


def per_device(grad, momentum, owner):
    size = lax.axis_size("tensor")
    new_momentum = decay * momentum + grad.astype(jnp.float32)
    direction = grad.astype(jnp.float32) + decay * new_momentum
    total = total_over(jnp.sum(direction * direction), "tensor", size)
    rows_here = (direction[0] / (jnp.sqrt(total) + eps)).astype(jnp.bfloat16)
    columns = lax.all_to_all(rows_here, "tensor", split_axis=1, concat_axis=0, tiled=True)
    for step in range(ITERS):
        partial = jnp.dot(columns, columns.T, preferred_element_type=jnp.float32)
        gram = gram_allreduce(partial, "tensor", size)
        square = jnp.dot(gram, gram, preferred_element_type=jnp.float32)
        poly = (coef_b * gram.astype(jnp.float32) + coef_c * square).astype(jnp.bfloat16)
        applied = jnp.dot(poly, columns, preferred_element_type=jnp.float32)
        columns = (coef_a * columns.astype(jnp.float32) + applied).astype(jnp.bfloat16)
    factor = 0.2 * math.sqrt(max(M, N))
    per = columns.shape[0] // size
    half = per // 2
    blocks = columns.reshape(size, per, columns.shape[1])
    slots = lax.axis_size("dp")
    ids = jnp.arange(slots, dtype=jnp.int32)
    inverse = jnp.sum(
        jnp.where(owner[None, :] == ids[:, None], ids[None, :], 0), axis=1
    )
    where_from = inverse ^ lax.axis_index("dp")
    pieces = []
    for lo, hi in ((0, half), (half, per)):
        piece = blocks[:, lo:hi, :].reshape(size * (hi - lo), columns.shape[1])
        back_rows = lax.all_to_all(piece, "tensor", split_axis=0, concat_axis=1, tiled=True)
        scaled = (factor * back_rows.astype(jnp.float32)).astype(jnp.bfloat16)
        held = gather_slots(scaled, "dp", slots)
        pieces.append(held)
    rows = []
    for m in range(slots):
        rows.append(
            jnp.concatenate(
                [lax.dynamic_index_in_dim(p, where_from[m], 0, keepdims=True) for p in pieces],
                axis=1,
            )
        )
    update = jnp.concatenate(rows, axis=0)
    return (update, new_momentum)


def solution(mesh):
    in_specs = (P("dp", "tensor", None), P("dp", "tensor", None), P())
    out_specs = (P(None, "tensor", None), P("dp", "tensor", None))
    return jax.shard_map(
        per_device, mesh=mesh, in_specs=in_specs, out_specs=out_specs, check_vma=False
    )
```

```python
import math

import jax
import jax.numpy as jnp
from jax import lax
from jax.sharding import PartitionSpec as P

M = 576
N = 6144
ITERS = 2


coef_a = 3.4445
coef_b = -4.775
coef_c = 2.0315
decay = 0.95
eps = 1e-07


def _shift_pairs(size, s):
    return [(i, (i + s) % size) for i in range(size)]


def total_over(value, axis, size):
    spread = jnp.broadcast_to(value, (size, 1))
    got = lax.all_to_all(spread, axis, split_axis=0, concat_axis=0, tiled=True)
    return jnp.sum(got)


def gram_allreduce(partial, axis, size):
    n = partial.shape[0]
    h = n // 2
    upper_a = partial[:h, :h]
    block_b = partial[:h, h:]
    lower_c = partial[h:, h:]
    row = lax.broadcasted_iota(jnp.int32, (h, h), 0)
    col = lax.broadcasted_iota(jnp.int32, (h, h), 1)
    folded = jnp.where(row <= col, upper_a, lower_c)
    diag_c = jnp.sum(jnp.where(row == col, lower_c, 0.0), axis=0)
    payload = jnp.concatenate([folded, block_b], axis=1)
    extra = jnp.concatenate([diag_c, jnp.zeros((h,), jnp.float32)])[None, :]
    rows = -(-(h + 1) // size) * size
    payload = jnp.concatenate(
        [payload, extra, jnp.zeros((rows - h - 1, 2 * h), jnp.float32)], axis=0
    )
    per = rows // size
    blocks = payload.reshape(size, per, 2 * h)
    me = lax.axis_index(axis)
    acc = lax.dynamic_index_in_dim(blocks, me, 0, keepdims=False)
    for s in range(1, size):
        outgoing = lax.dynamic_index_in_dim(blocks, (me + s) % size, 0, keepdims=False)
        acc = acc + lax.ppermute(outgoing, axis, _shift_pairs(size, s))
    mine = acc.astype(jnp.bfloat16)
    spread = jnp.broadcast_to(mine[None], (size,) + mine.shape)
    full = lax.all_to_all(spread, axis, split_axis=0, concat_axis=0, tiled=True).reshape(rows, 2 * h)
    folded_r = full[:h, :h]
    block_br = full[:h, h:]
    diag_cr = full[h, :h]
    upper_r = jnp.where(row <= col, folded_r, folded_r.T)
    lower_r = jnp.where(row > col, folded_r, folded_r.T)
    lower_r = jnp.where(row == col, diag_cr[None, :], lower_r)
    top = jnp.concatenate([upper_r, block_br], axis=1)
    bottom = jnp.concatenate([block_br.T, lower_r], axis=1)
    return jnp.concatenate([top, bottom], axis=0)


def gather_slots(mine, axis, size):
    if size & (size - 1) != 0:
        full = lax.all_gather(mine[None], axis, axis=0, tiled=True)
        me = lax.axis_index(axis)
        return jnp.take(full, jnp.arange(size, dtype=jnp.int32) ^ me, axis=0, mode="clip")
    held = {0: mine}
    bit = size // 2
    while bit >= 1:
        keys = sorted(held)
        sent = jnp.stack([held[j] for j in keys])
        got = lax.ppermute(sent, axis, [(i, i ^ bit) for i in range(size)])
        for n, j in enumerate(keys):
            held[j ^ bit] = got[n]
        bit //= 2
    return jnp.stack([held[j] for j in range(size)])


def per_device(grad, momentum, owner):
    size = lax.axis_size("tensor")
    new_momentum = decay * momentum + grad.astype(jnp.float32)
    direction = grad.astype(jnp.float32) + decay * new_momentum
    total = total_over(jnp.sum(direction * direction), "tensor", size)
    rows_here = (direction[0] / (jnp.sqrt(total) + eps)).astype(jnp.bfloat16)
    columns = lax.all_to_all(rows_here, "tensor", split_axis=1, concat_axis=0, tiled=True)
    for step in range(ITERS):
        partial = jnp.dot(columns, columns.T, preferred_element_type=jnp.float32)
        gram = gram_allreduce(partial, "tensor", size)
        square = jnp.dot(gram, gram, preferred_element_type=jnp.float32)
        poly = (coef_b * gram.astype(jnp.float32) + coef_c * square).astype(jnp.bfloat16)
        applied = jnp.dot(poly, columns, preferred_element_type=jnp.float32)
        columns = (coef_a * columns.astype(jnp.float32) + applied).astype(jnp.bfloat16)
    factor = 0.2 * math.sqrt(max(M, N))
    per = columns.shape[0] // size
    half = per // 2
    blocks = columns.reshape(size, per, columns.shape[1])
    slots = lax.axis_size("dp")
    ids = jnp.arange(slots, dtype=jnp.int32)
    inverse = jnp.sum(
        jnp.where(owner[None, :] == ids[:, None], ids[None, :], 0), axis=1
    )
    where_from = inverse ^ lax.axis_index("dp")
    pieces = []
    for lo, hi in ((0, half), (half, per)):
        piece = blocks[:, lo:hi, :].reshape(size * (hi - lo), columns.shape[1])
        back_rows = lax.all_to_all(piece, "tensor", split_axis=0, concat_axis=1, tiled=True)
        scaled = (factor * back_rows.astype(jnp.float32)).astype(jnp.bfloat16)
        held = gather_slots(scaled, "dp", slots)
        pieces.append(held)
    rows = []
    for m in range(slots):
        rows.append(
            jnp.concatenate(
                [lax.dynamic_index_in_dim(p, where_from[m], 0, keepdims=True) for p in pieces],
                axis=1,
            )
        )
    update = jnp.concatenate(rows, axis=0)
    return (update, new_momentum)


def solution(mesh):
    in_specs = (P("dp", "tensor", None), P("dp", "tensor", None), P())
    out_specs = (P(None, "tensor", None), P("dp", "tensor", None))
    return jax.shard_map(
        per_device, mesh=mesh, in_specs=in_specs, out_specs=out_specs, check_vma=False
    )
```

```python
import math

import jax
import jax.numpy as jnp
from jax import lax
from jax.sharding import PartitionSpec as P

M = 576
N = 6144
ITERS = 2


coef_a = 3.4445
coef_b = -4.775
coef_c = 2.0315
decay = 0.95
eps = 1e-07


def _shift_pairs(size, s):
    return [(i, (i + s) % size) for i in range(size)]


def total_over(value, axis, size):
    spread = jnp.broadcast_to(value, (size, 1))
    got = lax.all_to_all(spread, axis, split_axis=0, concat_axis=0, tiled=True)
    return jnp.sum(got)


def gram_allreduce(partial, axis, size):
    n = partial.shape[0]
    h = n // 2
    upper_a = partial[:h, :h]
    block_b = partial[:h, h:]
    lower_c = partial[h:, h:]
    row = lax.broadcasted_iota(jnp.int32, (h, h), 0)
    col = lax.broadcasted_iota(jnp.int32, (h, h), 1)
    folded = jnp.where(row <= col, upper_a, lower_c)
    diag_c = jnp.sum(jnp.where(row == col, lower_c, 0.0), axis=0)
    payload = jnp.concatenate([folded, block_b], axis=1)
    extra = jnp.concatenate([diag_c, jnp.zeros((h,), jnp.float32)])[None, :]
    rows = -(-(h + 1) // size) * size
    payload = jnp.concatenate(
        [payload, extra, jnp.zeros((rows - h - 1, 2 * h), jnp.float32)], axis=0
    )
    per = rows // size
    blocks = payload.reshape(size, per, 2 * h)
    me = lax.axis_index(axis)
    cut = 8 * (per // 16)
    chunks = [(0, cut), (cut, per)] if cut > 0 else [(0, per)]
    reduced = []
    for lo, hi in chunks:
        part = blocks[:, lo:hi, :]
        acc = lax.dynamic_index_in_dim(part, me, 0, keepdims=False)
        for s in range(1, size):
            outgoing = lax.dynamic_index_in_dim(part, (me + s) % size, 0, keepdims=False)
            acc = acc + lax.ppermute(outgoing, axis, _shift_pairs(size, s))
        reduced.append(acc.astype(jnp.bfloat16))
    pieces = []
    for mine in reduced:
        spread = jnp.broadcast_to(mine[None], (size,) + mine.shape)
        pieces.append(lax.all_to_all(spread, axis, split_axis=0, concat_axis=0, tiled=True))
    full = jnp.concatenate(pieces, axis=1).reshape(rows, 2 * h)
    folded_r = full[:h, :h]
    block_br = full[:h, h:]
    diag_cr = full[h, :h]
    upper_r = jnp.where(row <= col, folded_r, folded_r.T)
    lower_r = jnp.where(row > col, folded_r, folded_r.T)
    lower_r = jnp.where(row == col, diag_cr[None, :], lower_r)
    top = jnp.concatenate([upper_r, block_br], axis=1)
    bottom = jnp.concatenate([block_br.T, lower_r], axis=1)
    return jnp.concatenate([top, bottom], axis=0)


def gather_slots(mine, axis, size):
    if size & (size - 1) != 0:
        full = lax.all_gather(mine[None], axis, axis=0, tiled=True)
        me = lax.axis_index(axis)
        return jnp.take(full, jnp.arange(size, dtype=jnp.int32) ^ me, axis=0, mode="clip")
    held = {0: mine}
    bit = size // 2
    while bit >= 1:
        keys = sorted(held)
        sent = jnp.stack([held[j] for j in keys])
        got = lax.ppermute(sent, axis, [(i, i ^ bit) for i in range(size)])
        for n, j in enumerate(keys):
            held[j ^ bit] = got[n]
        bit //= 2
    return jnp.stack([held[j] for j in range(size)])


def per_device(grad, momentum, owner):
    size = lax.axis_size("tensor")
    new_momentum = decay * momentum + grad.astype(jnp.float32)
    direction = grad.astype(jnp.float32) + decay * new_momentum
    total = total_over(jnp.sum(direction * direction), "tensor", size)
    rows_here = (direction[0] / (jnp.sqrt(total) + eps)).astype(jnp.bfloat16)
    columns = lax.all_to_all(rows_here, "tensor", split_axis=1, concat_axis=0, tiled=True)
    for step in range(ITERS):
        partial = jnp.dot(columns, columns.T, preferred_element_type=jnp.float32)
        gram = gram_allreduce(partial, "tensor", size)
        square = jnp.dot(gram, gram, preferred_element_type=jnp.float32)
        poly = (coef_b * gram.astype(jnp.float32) + coef_c * square).astype(jnp.bfloat16)
        applied = jnp.dot(poly, columns, preferred_element_type=jnp.float32)
        columns = (coef_a * columns.astype(jnp.float32) + applied).astype(jnp.bfloat16)
    factor = 0.2 * math.sqrt(max(M, N))
    per = columns.shape[0] // size
    half = per // 2
    blocks = columns.reshape(size, per, columns.shape[1])
    slots = lax.axis_size("dp")
    ids = jnp.arange(slots, dtype=jnp.int32)
    inverse = jnp.sum(
        jnp.where(owner[None, :] == ids[:, None], ids[None, :], 0), axis=1
    )
    where_from = inverse ^ lax.axis_index("dp")
    pieces = []
    for lo, hi in ((0, half), (half, per)):
        piece = blocks[:, lo:hi, :].reshape(size * (hi - lo), columns.shape[1])
        back_rows = lax.all_to_all(piece, "tensor", split_axis=0, concat_axis=1, tiled=True)
        scaled = (factor * back_rows.astype(jnp.float32)).astype(jnp.bfloat16)
        held = gather_slots(scaled, "dp", slots)
        pieces.append(held)
    rows = []
    for m in range(slots):
        rows.append(
            jnp.concatenate(
                [lax.dynamic_index_in_dim(p, where_from[m], 0, keepdims=True) for p in pieces],
                axis=1,
            )
        )
    update = jnp.concatenate(rows, axis=0)
    return (update, new_momentum)


def solution(mesh):
    in_specs = (P("dp", "tensor", None), P("dp", "tensor", None), P())
    out_specs = (P(None, "tensor", None), P("dp", "tensor", None))
    return jax.shard_map(
        per_device, mesh=mesh, in_specs=in_specs, out_specs=out_specs, check_vma=False
    )
```

```python
import math

import jax
import jax.numpy as jnp
from jax import lax
from jax.sharding import PartitionSpec as P

M = 576
N = 6144
ITERS = 2


coef_a = 3.4445
coef_b = -4.775
coef_c = 2.0315
decay = 0.95
eps = 1e-07


def _shift_pairs(size, s):
    return [(i, (i + s) % size) for i in range(size)]


def total_over(value, axis, size):
    spread = jnp.broadcast_to(value, (size, 1))
    got = lax.all_to_all(spread, axis, split_axis=0, concat_axis=0, tiled=True)
    return jnp.sum(got)


def gram_allreduce(partial, axis, size):
    n = partial.shape[0]
    h = n // 2
    upper_a = partial[:h, :h]
    block_b = partial[:h, h:]
    lower_c = partial[h:, h:]
    row = lax.broadcasted_iota(jnp.int32, (h, h), 0)
    col = lax.broadcasted_iota(jnp.int32, (h, h), 1)
    folded = jnp.where(row <= col, upper_a, lower_c)
    diag_c = jnp.sum(jnp.where(row == col, lower_c, 0.0), axis=0)
    payload = jnp.concatenate([folded, block_b], axis=1)
    extra = jnp.concatenate([diag_c, jnp.zeros((h,), jnp.float32)])[None, :]
    rows = -(-(h + 1) // size) * size
    payload = jnp.concatenate(
        [payload, extra, jnp.zeros((rows - h - 1, 2 * h), jnp.float32)], axis=0
    )
    per = rows // size
    blocks = payload.reshape(size, per, 2 * h)
    me = lax.axis_index(axis)
    acc = lax.dynamic_index_in_dim(blocks, me, 0, keepdims=False)
    for s in range(1, size):
        outgoing = lax.dynamic_index_in_dim(blocks, (me + s) % size, 0, keepdims=False)
        acc = acc + lax.ppermute(outgoing, axis, _shift_pairs(size, s))
    mine = acc.astype(jnp.bfloat16)
    spread = jnp.broadcast_to(mine[None], (size,) + mine.shape)
    full = lax.all_to_all(spread, axis, split_axis=0, concat_axis=0, tiled=True).reshape(rows, 2 * h)
    folded_r = full[:h, :h]
    block_br = full[:h, h:]
    diag_cr = full[h, :h]
    upper_r = jnp.where(row <= col, folded_r, folded_r.T)
    lower_r = jnp.where(row > col, folded_r, folded_r.T)
    lower_r = jnp.where(row == col, diag_cr[None, :], lower_r)
    top = jnp.concatenate([upper_r, block_br], axis=1)
    bottom = jnp.concatenate([block_br.T, lower_r], axis=1)
    return jnp.concatenate([top, bottom], axis=0)


def gather_slots(mine, axis, size):
    if size & (size - 1) != 0:
        full = lax.all_gather(mine[None], axis, axis=0, tiled=True)
        me = lax.axis_index(axis)
        for j in range(size):
            yield j, lax.dynamic_index_in_dim(full, me ^ j, 0, keepdims=False)
        return
    yield 0, mine
    held = {0: mine}
    bit = size // 2
    while bit >= 1:
        keys = sorted(held)
        sent = jnp.stack([held[j] for j in keys])
        got = lax.ppermute(sent, axis, [(i, i ^ bit) for i in range(size)])
        for n, j in enumerate(keys):
            held[j ^ bit] = got[n]
            yield j ^ bit, got[n]
        bit //= 2


def per_device(grad, momentum, owner):
    size = lax.axis_size("tensor")
    new_momentum = decay * momentum + grad.astype(jnp.float32)
    direction = grad.astype(jnp.float32) + decay * new_momentum
    total = total_over(jnp.sum(direction * direction), "tensor", size)
    rows_here = (direction[0] / (jnp.sqrt(total) + eps)).astype(jnp.bfloat16)
    columns = lax.all_to_all(rows_here, "tensor", split_axis=1, concat_axis=0, tiled=True)
    for step in range(ITERS):
        partial = jnp.dot(columns, columns.T, preferred_element_type=jnp.float32)
        gram = gram_allreduce(partial, "tensor", size)
        square = jnp.dot(gram, gram, preferred_element_type=jnp.float32)
        poly = (coef_b * gram.astype(jnp.float32) + coef_c * square).astype(jnp.bfloat16)
        applied = jnp.dot(poly, columns, preferred_element_type=jnp.float32)
        columns = (coef_a * columns.astype(jnp.float32) + applied).astype(jnp.bfloat16)
    factor = 0.2 * math.sqrt(max(M, N))
    per = columns.shape[0] // size
    half = per // 2
    blocks = columns.reshape(size, per, columns.shape[1])
    slots = lax.axis_size("dp")
    me_dp = lax.axis_index("dp")
    update = jnp.zeros((slots, per, size * columns.shape[1]), jnp.bfloat16)
    for lo, hi in ((0, half), (half, per)):
        piece = blocks[:, lo:hi, :].reshape(size * (hi - lo), columns.shape[1])
        back_rows = lax.all_to_all(piece, "tensor", split_axis=0, concat_axis=1, tiled=True)
        scaled = (factor * back_rows.astype(jnp.float32)).astype(jnp.bfloat16)
        for j, block in gather_slots(scaled, "dp", slots):
            update = lax.dynamic_update_slice(update, block[None], (owner[me_dp ^ j], lo, 0))
    return (update, new_momentum)


def solution(mesh):
    in_specs = (P("dp", "tensor", None), P("dp", "tensor", None), P())
    out_specs = (P(None, "tensor", None), P("dp", "tensor", None))
    return jax.shard_map(
        per_device, mesh=mesh, in_specs=in_specs, out_specs=out_specs, check_vma=False
    )
```

```python
import math

import jax
import jax.numpy as jnp
from jax import lax
from jax.sharding import PartitionSpec as P

M = 576
N = 6144
ITERS = 2


coef_a = 3.4445
coef_b = -4.775
coef_c = 2.0315
decay = 0.95
eps = 1e-07


def _shift_pairs(size, s):
    return [(i, (i + s) % size) for i in range(size)]


def total_over(value, axis, size):
    spread = jnp.broadcast_to(value, (size, 1))
    got = lax.all_to_all(spread, axis, split_axis=0, concat_axis=0, tiled=True)
    return jnp.sum(got)


def gram_allreduce(partial, axis, size):
    n = partial.shape[0]
    h = n // 2
    upper_a = partial[:h, :h]
    block_b = partial[:h, h:]
    lower_c = partial[h:, h:]
    row = lax.broadcasted_iota(jnp.int32, (h, h), 0)
    col = lax.broadcasted_iota(jnp.int32, (h, h), 1)
    folded = jnp.where(row <= col, upper_a, lower_c)
    diag_c = jnp.sum(jnp.where(row == col, lower_c, 0.0), axis=0)
    payload = jnp.concatenate([folded, block_b], axis=1)
    extra = jnp.concatenate([diag_c, jnp.zeros((h,), jnp.float32)])[None, :]
    rows = -(-(h + 1) // size) * size
    payload = jnp.concatenate(
        [payload, extra, jnp.zeros((rows - h - 1, 2 * h), jnp.float32)], axis=0
    )
    per = rows // size
    blocks = payload.reshape(size, per, 2 * h)
    me = lax.axis_index(axis)
    acc = lax.dynamic_index_in_dim(blocks, me, 0, keepdims=False)
    for s in range(1, size):
        outgoing = lax.dynamic_index_in_dim(blocks, (me + s) % size, 0, keepdims=False)
        acc = acc + lax.ppermute(outgoing, axis, _shift_pairs(size, s))
    mine = acc.astype(jnp.bfloat16)
    spread = jnp.broadcast_to(mine[None], (size,) + mine.shape)
    full = lax.all_to_all(spread, axis, split_axis=0, concat_axis=0, tiled=True).reshape(rows, 2 * h)
    folded_r = full[:h, :h]
    block_br = full[:h, h:]
    diag_cr = full[h, :h]
    upper_r = jnp.where(row <= col, folded_r, folded_r.T)
    lower_r = jnp.where(row > col, folded_r, folded_r.T)
    lower_r = jnp.where(row == col, diag_cr[None, :], lower_r)
    top = jnp.concatenate([upper_r, block_br], axis=1)
    bottom = jnp.concatenate([block_br.T, lower_r], axis=1)
    return jnp.concatenate([top, bottom], axis=0)


def gather_slots(mine, axis, size):
    if size & (size - 1) != 0:
        full = lax.all_gather(mine[None], axis, axis=0, tiled=True)
        me = lax.axis_index(axis)
        return jnp.take(full, jnp.arange(size, dtype=jnp.int32) ^ me, axis=0, mode="clip")
    held = {0: mine}
    bit = size // 2
    while bit >= 1:
        keys = sorted(held)
        sent = jnp.stack([held[j] for j in keys])
        got = lax.ppermute(sent, axis, [(i, i ^ bit) for i in range(size)])
        for n, j in enumerate(keys):
            held[j ^ bit] = got[n]
        bit //= 2
    return jnp.stack([held[j] for j in range(size)])


def per_device(grad, momentum, owner):
    size = lax.axis_size("tensor")
    new_momentum = decay * momentum + grad.astype(jnp.float32)
    direction = grad.astype(jnp.float32) + decay * new_momentum
    total = total_over(jnp.sum(direction * direction), "tensor", size)
    rows_here = (direction[0] / (jnp.sqrt(total) + eps)).astype(jnp.bfloat16)
    columns = lax.all_to_all(rows_here, "tensor", split_axis=1, concat_axis=0, tiled=True)
    for step in range(ITERS):
        partial = jnp.dot(columns, columns.T, preferred_element_type=jnp.float32)
        gram = gram_allreduce(partial, "tensor", size)
        square = jnp.dot(gram, gram, preferred_element_type=jnp.float32)
        poly = (coef_b * gram.astype(jnp.float32) + coef_c * square).astype(jnp.bfloat16)
        applied = jnp.dot(poly, columns, preferred_element_type=jnp.float32)
        columns = (coef_a * columns.astype(jnp.float32) + applied).astype(jnp.bfloat16)
    factor = 0.2 * math.sqrt(max(M, N))
    per = columns.shape[0] // size
    half = min(per, 8 * ((per * 9 + 64) // 128))
    blocks = columns.reshape(size, per, columns.shape[1])
    slots = lax.axis_size("dp")
    ids = jnp.arange(slots, dtype=jnp.int32)
    inverse = jnp.sum(
        jnp.where(owner[None, :] == ids[:, None], ids[None, :], 0), axis=1
    )
    where_from = inverse ^ lax.axis_index("dp")
    pieces = []
    for lo, hi in ((0, half), (half, per)) if half < per else ((0, per),):
        piece = blocks[:, lo:hi, :].reshape(size * (hi - lo), columns.shape[1])
        back_rows = lax.all_to_all(piece, "tensor", split_axis=0, concat_axis=1, tiled=True)
        scaled = (factor * back_rows.astype(jnp.float32)).astype(jnp.bfloat16)
        held = gather_slots(scaled, "dp", slots)
        pieces.append(held)
    rows = []
    for m in range(slots):
        rows.append(
            jnp.concatenate(
                [lax.dynamic_index_in_dim(p, where_from[m], 0, keepdims=True) for p in pieces],
                axis=1,
            )
        )
    update = jnp.concatenate(rows, axis=0)
    return (update, new_momentum)


def solution(mesh):
    in_specs = (P("dp", "tensor", None), P("dp", "tensor", None), P())
    out_specs = (P(None, "tensor", None), P("dp", "tensor", None))
    return jax.shard_map(
        per_device, mesh=mesh, in_specs=in_specs, out_specs=out_specs, check_vma=False
    )
```

```python
import math

import jax
import jax.numpy as jnp
from jax import lax
from jax.sharding import PartitionSpec as P

M = 576
N = 6144
ITERS = 2


coef_a = 3.4445
coef_b = -4.775
coef_c = 2.0315
decay = 0.95
eps = 1e-07


def _shift_pairs(size, s):
    return [(i, (i + s) % size) for i in range(size)]


def total_over(value, axis, size):
    spread = jnp.broadcast_to(value, (size, 1))
    got = lax.all_to_all(spread, axis, split_axis=0, concat_axis=0, tiled=True)
    return jnp.sum(got)


def gram_allreduce(partial, axis, size):
    n = partial.shape[0]
    h = n // 2
    upper_a = partial[:h, :h]
    block_b = partial[:h, h:]
    lower_c = partial[h:, h:]
    row = lax.broadcasted_iota(jnp.int32, (h, h), 0)
    col = lax.broadcasted_iota(jnp.int32, (h, h), 1)
    folded = jnp.where(row <= col, upper_a, lower_c)
    diag_c = jnp.sum(jnp.where(row == col, lower_c, 0.0), axis=0)
    payload = jnp.concatenate([folded, block_b], axis=1)
    extra = jnp.concatenate([diag_c, jnp.zeros((h,), jnp.float32)])[None, :]
    rows = -(-(h + 1) // size) * size
    payload = jnp.concatenate(
        [payload, extra, jnp.zeros((rows - h - 1, 2 * h), jnp.float32)], axis=0
    )
    per = rows // size
    blocks = payload.reshape(size, per, 2 * h)
    me = lax.axis_index(axis)
    acc = lax.dynamic_index_in_dim(blocks, me, 0, keepdims=False)
    for s in range(1, size):
        outgoing = lax.dynamic_index_in_dim(blocks, (me + s) % size, 0, keepdims=False)
        acc = acc + lax.ppermute(outgoing, axis, _shift_pairs(size, s))
    mine = acc.astype(jnp.bfloat16)
    spread = jnp.broadcast_to(mine[None], (size,) + mine.shape)
    full = lax.all_to_all(spread, axis, split_axis=0, concat_axis=0, tiled=True).reshape(rows, 2 * h)
    folded_r = full[:h, :h]
    block_br = full[:h, h:]
    diag_cr = full[h, :h]
    upper_r = jnp.where(row <= col, folded_r, folded_r.T)
    lower_r = jnp.where(row > col, folded_r, folded_r.T)
    lower_r = jnp.where(row == col, diag_cr[None, :], lower_r)
    top = jnp.concatenate([upper_r, block_br], axis=1)
    bottom = jnp.concatenate([block_br.T, lower_r], axis=1)
    return jnp.concatenate([top, bottom], axis=0)


def gather_slots(mine, axis, size):
    if size & (size - 1) != 0:
        full = lax.all_gather(mine[None], axis, axis=0, tiled=True)
        me = lax.axis_index(axis)
        return jnp.take(full, jnp.arange(size, dtype=jnp.int32) ^ me, axis=0, mode="clip")
    held = {0: mine}
    bit = size // 2
    while bit >= 1:
        keys = sorted(held)
        sent = jnp.stack([held[j] for j in keys])
        got = lax.ppermute(sent, axis, [(i, i ^ bit) for i in range(size)])
        for n, j in enumerate(keys):
            held[j ^ bit] = got[n]
        bit //= 2
    return jnp.stack([held[j] for j in range(size)])


def per_device(grad, momentum, owner):
    size = lax.axis_size("tensor")
    new_momentum = decay * momentum + grad.astype(jnp.float32)
    direction = grad.astype(jnp.float32) + decay * new_momentum
    total = total_over(jnp.sum(direction * direction), "tensor", size)
    rows_here = (direction[0] / (jnp.sqrt(total) + eps)).astype(jnp.bfloat16)
    columns = lax.all_to_all(rows_here, "tensor", split_axis=1, concat_axis=0, tiled=True)
    for step in range(ITERS):
        partial = jnp.dot(columns, columns.T, preferred_element_type=jnp.float32)
        gram = gram_allreduce(partial, "tensor", size)
        square = jnp.dot(gram, gram, preferred_element_type=jnp.float32)
        poly = (coef_b * gram.astype(jnp.float32) + coef_c * square).astype(jnp.bfloat16)
        applied = jnp.dot(poly, columns, preferred_element_type=jnp.float32)
        columns = (coef_a * columns.astype(jnp.float32) + applied).astype(jnp.bfloat16)
    factor = 0.2 * math.sqrt(max(M, N))
    per = columns.shape[0] // size
    half = min(per, 8 * ((per * 9 + 64) // 128))
    blocks = columns.reshape(size, per, columns.shape[1])
    slots = lax.axis_size("dp")
    ids = jnp.arange(slots, dtype=jnp.int32)
    inverse = jnp.sum(
        jnp.where(owner[None, :] == ids[:, None], ids[None, :], 0), axis=1
    )
    where_from = inverse ^ lax.axis_index("dp")
    bounds = ((0, half), (half, per)) if half < per else ((0, per),)
    parts = [
        blocks[:, lo:hi, :].reshape(size * (hi - lo), columns.shape[1]) for lo, hi in bounds
    ]
    pieces = []
    for n in range(len(parts)):
        back_rows = lax.all_to_all(parts[n], "tensor", split_axis=0, concat_axis=1, tiled=True)
        if n + 1 < len(parts):
            parts[n + 1], back_rows = lax.optimization_barrier((parts[n + 1], back_rows))
        scaled = (factor * back_rows.astype(jnp.float32)).astype(jnp.bfloat16)
        pieces.append(gather_slots(scaled, "dp", slots))
    rows = []
    for m in range(slots):
        rows.append(
            jnp.concatenate(
                [lax.dynamic_index_in_dim(p, where_from[m], 0, keepdims=True) for p in pieces],
                axis=1,
            )
        )
    update = jnp.concatenate(rows, axis=0)
    return (update, new_momentum)


def solution(mesh):
    in_specs = (P("dp", "tensor", None), P("dp", "tensor", None), P())
    out_specs = (P(None, "tensor", None), P("dp", "tensor", None))
    return jax.shard_map(
        per_device, mesh=mesh, in_specs=in_specs, out_specs=out_specs, check_vma=False
    )
```

```python
import math

import jax
import jax.numpy as jnp
from jax import lax
from jax.sharding import PartitionSpec as P

M = 576
N = 6144
ITERS = 2


coef_a = 3.4445
coef_b = -4.775
coef_c = 2.0315
decay = 0.95
eps = 1e-07


def _shift_pairs(size, s):
    return [(i, (i + s) % size) for i in range(size)]


def total_over(value, axis, size):
    spread = jnp.broadcast_to(value, (size, 1))
    got = lax.all_to_all(spread, axis, split_axis=0, concat_axis=0, tiled=True)
    return jnp.sum(got)


def gram_allreduce(partial, axis, size):
    n = partial.shape[0]
    h = n // 2
    upper_a = partial[:h, :h]
    block_b = partial[:h, h:]
    lower_c = partial[h:, h:]
    row = lax.broadcasted_iota(jnp.int32, (h, h), 0)
    col = lax.broadcasted_iota(jnp.int32, (h, h), 1)
    folded = jnp.where(row <= col, upper_a, lower_c)
    diag_c = jnp.sum(jnp.where(row == col, lower_c, 0.0), axis=0)
    payload = jnp.concatenate([folded, block_b], axis=1)
    extra = jnp.concatenate([diag_c, jnp.zeros((h,), jnp.float32)])[None, :]
    rows = -(-(h + 1) // size) * size
    payload = jnp.concatenate(
        [payload, extra, jnp.zeros((rows - h - 1, 2 * h), jnp.float32)], axis=0
    )
    per = rows // size
    blocks = payload.reshape(size, per, 2 * h)
    received = lax.all_to_all(blocks, axis, split_axis=0, concat_axis=0, tiled=True)
    acc = received[0]
    for s in range(1, size):
        acc = acc + received[s]
    mine = acc.astype(jnp.bfloat16)
    spread = jnp.broadcast_to(mine[None], (size,) + mine.shape)
    full = lax.all_to_all(spread, axis, split_axis=0, concat_axis=0, tiled=True).reshape(rows, 2 * h)
    folded_r = full[:h, :h]
    block_br = full[:h, h:]
    diag_cr = full[h, :h]
    upper_r = jnp.where(row <= col, folded_r, folded_r.T)
    lower_r = jnp.where(row > col, folded_r, folded_r.T)
    lower_r = jnp.where(row == col, diag_cr[None, :], lower_r)
    top = jnp.concatenate([upper_r, block_br], axis=1)
    bottom = jnp.concatenate([block_br.T, lower_r], axis=1)
    return jnp.concatenate([top, bottom], axis=0)


def gather_slots(mine, axis, size):
    if size & (size - 1) != 0:
        full = lax.all_gather(mine[None], axis, axis=0, tiled=True)
        me = lax.axis_index(axis)
        return jnp.take(full, jnp.arange(size, dtype=jnp.int32) ^ me, axis=0, mode="clip")
    held = {0: mine}
    bit = size // 2
    while bit >= 1:
        keys = sorted(held)
        sent = jnp.stack([held[j] for j in keys])
        got = lax.ppermute(sent, axis, [(i, i ^ bit) for i in range(size)])
        for n, j in enumerate(keys):
            held[j ^ bit] = got[n]
        bit //= 2
    return jnp.stack([held[j] for j in range(size)])


def per_device(grad, momentum, owner):
    size = lax.axis_size("tensor")
    new_momentum = decay * momentum + grad.astype(jnp.float32)
    direction = grad.astype(jnp.float32) + decay * new_momentum
    total = total_over(jnp.sum(direction * direction), "tensor", size)
    rows_here = (direction[0] / (jnp.sqrt(total) + eps)).astype(jnp.bfloat16)
    columns = lax.all_to_all(rows_here, "tensor", split_axis=1, concat_axis=0, tiled=True)
    for step in range(ITERS):
        partial = jnp.dot(columns, columns.T, preferred_element_type=jnp.float32)
        gram = gram_allreduce(partial, "tensor", size)
        square = jnp.dot(gram, gram, preferred_element_type=jnp.float32)
        poly = (coef_b * gram.astype(jnp.float32) + coef_c * square).astype(jnp.bfloat16)
        applied = jnp.dot(poly, columns, preferred_element_type=jnp.float32)
        columns = (coef_a * columns.astype(jnp.float32) + applied).astype(jnp.bfloat16)
    factor = 0.2 * math.sqrt(max(M, N))
    per = columns.shape[0] // size
    half = min(per, 8 * ((per * 9 + 64) // 128))
    blocks = columns.reshape(size, per, columns.shape[1])
    slots = lax.axis_size("dp")
    ids = jnp.arange(slots, dtype=jnp.int32)
    inverse = jnp.sum(
        jnp.where(owner[None, :] == ids[:, None], ids[None, :], 0), axis=1
    )
    where_from = inverse ^ lax.axis_index("dp")
    bounds = ((0, half), (half, per)) if half < per else ((0, per),)
    parts = [
        blocks[:, lo:hi, :].reshape(size * (hi - lo), columns.shape[1]) for lo, hi in bounds
    ]
    pieces = []
    for n in range(len(parts)):
        back_rows = lax.all_to_all(parts[n], "tensor", split_axis=0, concat_axis=1, tiled=True)
        if n + 1 < len(parts):
            parts[n + 1], back_rows = lax.optimization_barrier((parts[n + 1], back_rows))
        scaled = (factor * back_rows.astype(jnp.float32)).astype(jnp.bfloat16)
        pieces.append(gather_slots(scaled, "dp", slots))
    rows = []
    for m in range(slots):
        rows.append(
            jnp.concatenate(
                [lax.dynamic_index_in_dim(p, where_from[m], 0, keepdims=True) for p in pieces],
                axis=1,
            )
        )
    update = jnp.concatenate(rows, axis=0)
    return (update, new_momentum)


def solution(mesh):
    in_specs = (P("dp", "tensor", None), P("dp", "tensor", None), P())
    out_specs = (P(None, "tensor", None), P("dp", "tensor", None))
    return jax.shard_map(
        per_device, mesh=mesh, in_specs=in_specs, out_specs=out_specs, check_vma=False
    )
```

```python
import math

import jax
import jax.numpy as jnp
from jax import lax
from jax.sharding import PartitionSpec as P

M = 576
N = 6144
ITERS = 2


coef_a = 3.4445
coef_b = -4.775
coef_c = 2.0315
decay = 0.95
eps = 1e-07


def _shift_pairs(size, s):
    return [(i, (i + s) % size) for i in range(size)]


def total_over(value, axis, size):
    spread = jnp.broadcast_to(value, (size, 1))
    got = lax.all_to_all(spread, axis, split_axis=0, concat_axis=0, tiled=True)
    return jnp.sum(got)


def gram_allreduce(partial, axis, size):
    n = partial.shape[0]
    h = n // 2
    upper_a = partial[:h, :h]
    block_b = partial[:h, h:]
    lower_c = partial[h:, h:]
    row = lax.broadcasted_iota(jnp.int32, (h, h), 0)
    col = lax.broadcasted_iota(jnp.int32, (h, h), 1)
    folded = jnp.where(row <= col, upper_a, lower_c)
    diag_c = jnp.sum(jnp.where(row == col, lower_c, 0.0), axis=0)
    payload = jnp.concatenate([folded, block_b], axis=1)
    extra = jnp.concatenate([diag_c, jnp.zeros((h,), jnp.float32)])[None, :]
    rows = -(-(h + 1) // size) * size
    payload = jnp.concatenate(
        [payload, extra, jnp.zeros((rows - h - 1, 2 * h), jnp.float32)], axis=0
    )
    per = rows // size
    blocks = payload.reshape(size, per, 2 * h)
    me = lax.axis_index(axis)
    acc = lax.dynamic_index_in_dim(blocks, me, 0, keepdims=False)
    for s in range(1, size):
        outgoing = lax.dynamic_index_in_dim(blocks, (me + s) % size, 0, keepdims=False)
        acc = acc + lax.ppermute(outgoing, axis, _shift_pairs(size, s))
    mine = acc.astype(jnp.bfloat16)
    spread = jnp.broadcast_to(mine[None], (size,) + mine.shape)
    full = lax.all_to_all(spread, axis, split_axis=0, concat_axis=0, tiled=True).reshape(rows, 2 * h)
    folded_r = full[:h, :h]
    block_br = full[:h, h:]
    diag_cr = full[h, :h]
    upper_r = jnp.where(row <= col, folded_r, folded_r.T)
    lower_r = jnp.where(row > col, folded_r, folded_r.T)
    lower_r = jnp.where(row == col, diag_cr[None, :], lower_r)
    top = jnp.concatenate([upper_r, block_br], axis=1)
    bottom = jnp.concatenate([block_br.T, lower_r], axis=1)
    return jnp.concatenate([top, bottom], axis=0)


def gather_slots(mine, axis, size):
    if size & (size - 1) != 0:
        full = lax.all_gather(mine[None], axis, axis=0, tiled=True)
        me = lax.axis_index(axis)
        return jnp.take(full, jnp.arange(size, dtype=jnp.int32) ^ me, axis=0, mode="clip")
    held = {0: mine}
    bit = size // 2
    while bit >= 1:
        keys = sorted(held)
        sent = jnp.stack([held[j] for j in keys])
        got = lax.ppermute(sent, axis, [(i, i ^ bit) for i in range(size)])
        for n, j in enumerate(keys):
            held[j ^ bit] = got[n]
        bit //= 2
    return jnp.stack([held[j] for j in range(size)])


def per_device(grad, momentum, owner):
    size = lax.axis_size("tensor")
    new_momentum = decay * momentum + grad.astype(jnp.float32)
    direction = grad.astype(jnp.float32) + decay * new_momentum
    total = total_over(jnp.sum(direction * direction), "tensor", size)
    rows_here = (direction[0] / (jnp.sqrt(total) + eps)).astype(jnp.bfloat16)
    columns = lax.all_to_all(rows_here, "tensor", split_axis=1, concat_axis=0, tiled=True)
    for step in range(ITERS):
        partial = jnp.dot(columns, columns.T, preferred_element_type=jnp.float32)
        gram = gram_allreduce(partial, "tensor", size)
        square = jnp.dot(gram, gram, preferred_element_type=jnp.float32)
        poly = (coef_b * gram.astype(jnp.float32) + coef_c * square).astype(jnp.bfloat16)
        applied = jnp.dot(poly, columns, preferred_element_type=jnp.float32)
        columns = (coef_a * columns.astype(jnp.float32) + applied).astype(jnp.bfloat16)
    factor = 0.2 * math.sqrt(max(M, N))
    per = columns.shape[0] // size
    blocks = columns.reshape(size, per, columns.shape[1])
    slots = lax.axis_size("dp")
    ids = jnp.arange(slots, dtype=jnp.int32)
    inverse = jnp.sum(
        jnp.where(owner[None, :] == ids[:, None], ids[None, :], 0), axis=1
    )
    where_from = inverse ^ lax.axis_index("dp")
    bounds = []
    lo = 0
    for share in (4, 3):
        hi = min(per, lo + 8 * ((per * share + 36) // 72))
        if lo < hi < per:
            bounds.append((lo, hi))
            lo = hi
    bounds.append((lo, per))
    parts = [
        blocks[:, lo:hi, :].reshape(size * (hi - lo), columns.shape[1]) for lo, hi in bounds
    ]
    pieces = []
    for n in range(len(parts)):
        back_rows = lax.all_to_all(parts[n], "tensor", split_axis=0, concat_axis=1, tiled=True)
        if n + 1 < len(parts):
            parts[n + 1], back_rows = lax.optimization_barrier((parts[n + 1], back_rows))
        scaled = (factor * back_rows.astype(jnp.float32)).astype(jnp.bfloat16)
        pieces.append(gather_slots(scaled, "dp", slots))
    rows = []
    for m in range(slots):
        rows.append(
            jnp.concatenate(
                [lax.dynamic_index_in_dim(p, where_from[m], 0, keepdims=True) for p in pieces],
                axis=1,
            )
        )
    update = jnp.concatenate(rows, axis=0)
    return (update, new_momentum)


def solution(mesh):
    in_specs = (P("dp", "tensor", None), P("dp", "tensor", None), P())
    out_specs = (P(None, "tensor", None), P("dp", "tensor", None))
    return jax.shard_map(
        per_device, mesh=mesh, in_specs=in_specs, out_specs=out_specs, check_vma=False
    )
```

```python
import math

import jax
import jax.numpy as jnp
from jax import lax
from jax.sharding import PartitionSpec as P

M = 576
N = 6144
ITERS = 2


coef_a = 3.4445
coef_b = -4.775
coef_c = 2.0315
decay = 0.95
eps = 1e-07


def _shift_pairs(size, s):
    return [(i, (i + s) % size) for i in range(size)]


def total_over(value, axis, size):
    spread = jnp.broadcast_to(value, (size, 1))
    got = lax.all_to_all(spread, axis, split_axis=0, concat_axis=0, tiled=True)
    return jnp.sum(got)


def gram_allreduce(partial, axis, size):
    n = partial.shape[0]
    h = n // 2
    upper_a = partial[:h, :h]
    block_b = partial[:h, h:]
    lower_c = partial[h:, h:]
    row = lax.broadcasted_iota(jnp.int32, (h, h), 0)
    col = lax.broadcasted_iota(jnp.int32, (h, h), 1)
    folded = jnp.where(row <= col, upper_a, lower_c)
    diag_c = jnp.sum(jnp.where(row == col, lower_c, 0.0), axis=0)
    payload = jnp.concatenate([folded, block_b], axis=1)
    extra = jnp.concatenate([diag_c, jnp.zeros((h,), jnp.float32)])[None, :]
    rows = -(-(h + 1) // size) * size
    payload = jnp.concatenate(
        [payload, extra, jnp.zeros((rows - h - 1, 2 * h), jnp.float32)], axis=0
    )
    per = rows // size
    blocks = payload.reshape(size, per, 2 * h)
    me = lax.axis_index(axis)
    acc = lax.dynamic_index_in_dim(blocks, me, 0, keepdims=False)
    for s in range(1, size):
        outgoing = lax.dynamic_index_in_dim(blocks, (me + s) % size, 0, keepdims=False)
        acc = acc + lax.ppermute(outgoing, axis, _shift_pairs(size, s))
    mine = acc.astype(jnp.bfloat16)
    spread = jnp.broadcast_to(mine[None], (size,) + mine.shape)
    full = lax.all_to_all(spread, axis, split_axis=0, concat_axis=0, tiled=True).reshape(rows, 2 * h)
    folded_r = full[:h, :h]
    block_br = full[:h, h:]
    diag_cr = full[h, :h]
    upper_r = jnp.where(row <= col, folded_r, folded_r.T)
    lower_r = jnp.where(row > col, folded_r, folded_r.T)
    lower_r = jnp.where(row == col, diag_cr[None, :], lower_r)
    top = jnp.concatenate([upper_r, block_br], axis=1)
    bottom = jnp.concatenate([block_br.T, lower_r], axis=1)
    return jnp.concatenate([top, bottom], axis=0)


def gather_slots(mine, axis, size):
    if size & (size - 1) != 0:
        full = lax.all_gather(mine[None], axis, axis=0, tiled=True)
        me = lax.axis_index(axis)
        return jnp.take(full, jnp.arange(size, dtype=jnp.int32) ^ me, axis=0, mode="clip")
    return gather_slots_from({0: mine}, axis, size, size // 2)


def gather_slots_from(held, axis, size, bit):
    held = dict(held)
    while bit >= 1:
        keys = sorted(held)
        sent = jnp.stack([held[j] for j in keys])
        got = lax.ppermute(sent, axis, [(i, i ^ bit) for i in range(size)])
        for n, j in enumerate(keys):
            held[j ^ bit] = got[n]
        bit //= 2
    return jnp.stack([held[j] for j in range(size)])


def per_device(grad, momentum, owner):
    size = lax.axis_size("tensor")
    new_momentum = decay * momentum + grad.astype(jnp.float32)
    direction = grad.astype(jnp.float32) + decay * new_momentum
    total = total_over(jnp.sum(direction * direction), "tensor", size)
    rows_here = (direction[0] / (jnp.sqrt(total) + eps)).astype(jnp.bfloat16)
    columns = lax.all_to_all(rows_here, "tensor", split_axis=1, concat_axis=0, tiled=True)
    for step in range(ITERS):
        partial = jnp.dot(columns, columns.T, preferred_element_type=jnp.float32)
        gram = gram_allreduce(partial, "tensor", size)
        square = jnp.dot(gram, gram, preferred_element_type=jnp.float32)
        poly = (coef_b * gram.astype(jnp.float32) + coef_c * square).astype(jnp.bfloat16)
        applied = jnp.dot(poly, columns, preferred_element_type=jnp.float32)
        columns = (coef_a * columns.astype(jnp.float32) + applied).astype(jnp.bfloat16)
    factor = 0.2 * math.sqrt(max(M, N))
    per = columns.shape[0] // size
    half = min(per, 8 * ((per * 2 + 12) // 24))
    blocks = columns.reshape(size, per, columns.shape[1])
    slots = lax.axis_size("dp")
    ids = jnp.arange(slots, dtype=jnp.int32)
    inverse = jnp.sum(
        jnp.where(owner[None, :] == ids[:, None], ids[None, :], 0), axis=1
    )
    where_from = inverse ^ lax.axis_index("dp")
    cut = half if half < per else per
    hb = slots // 2
    pieces = []
    first = blocks[:, :cut, :].reshape(size * cut, columns.shape[1])
    if cut < per and slots > 1 and slots & (slots - 1) == 0:
        late = blocks[:, cut:, :]
        partner = lax.ppermute(late, "dp", [(i, i ^ hb) for i in range(slots)])
    back_rows = lax.all_to_all(first, "tensor", split_axis=0, concat_axis=1, tiled=True)
    scaled = (factor * back_rows.astype(jnp.float32)).astype(jnp.bfloat16)
    pieces.append(gather_slots(scaled, "dp", slots))
    if cut < per and slots > 1 and slots & (slots - 1) == 0:
        both = jnp.stack([late, partner], axis=1).reshape(size * 2 * (per - cut), columns.shape[1])
        back_rows = lax.all_to_all(both, "tensor", split_axis=0, concat_axis=1, tiled=True)
        scaled = (factor * back_rows.astype(jnp.float32)).astype(jnp.bfloat16)
        scaled = scaled.reshape(2, per - cut, scaled.shape[1])
        pieces.append(gather_slots_from({0: scaled[0], hb: scaled[1]}, "dp", slots, hb // 2))
    elif cut < per:
        rest = blocks[:, cut:, :].reshape(size * (per - cut), columns.shape[1])
        back_rows = lax.all_to_all(rest, "tensor", split_axis=0, concat_axis=1, tiled=True)
        scaled = (factor * back_rows.astype(jnp.float32)).astype(jnp.bfloat16)
        pieces.append(gather_slots(scaled, "dp", slots))
    rows = []
    for m in range(slots):
        rows.append(
            jnp.concatenate(
                [lax.dynamic_index_in_dim(p, where_from[m], 0, keepdims=True) for p in pieces],
                axis=1,
            )
        )
    update = jnp.concatenate(rows, axis=0)
    return (update, new_momentum)


def solution(mesh):
    in_specs = (P("dp", "tensor", None), P("dp", "tensor", None), P())
    out_specs = (P(None, "tensor", None), P("dp", "tensor", None))
    return jax.shard_map(
        per_device, mesh=mesh, in_specs=in_specs, out_specs=out_specs, check_vma=False
    )
```

```python
import math

import jax
import jax.numpy as jnp
from jax import lax
from jax.sharding import PartitionSpec as P

M = 576
N = 6144
ITERS = 2


coef_a = 3.4445
coef_b = -4.775
coef_c = 2.0315
decay = 0.95
eps = 1e-07


def _shift_pairs(size, s):
    return [(i, (i + s) % size) for i in range(size)]


def total_over(value, axis, size):
    spread = jnp.broadcast_to(value, (size, 1))
    got = lax.all_to_all(spread, axis, split_axis=0, concat_axis=0, tiled=True)
    return jnp.sum(got)


def gram_allreduce(partial, axis, size):
    n = partial.shape[0]
    h = n // 2
    upper_a = partial[:h, :h]
    block_b = partial[:h, h:]
    lower_c = partial[h:, h:]
    row = lax.broadcasted_iota(jnp.int32, (h, h), 0)
    col = lax.broadcasted_iota(jnp.int32, (h, h), 1)
    folded = jnp.where(row <= col, upper_a, lower_c)
    diag_c = jnp.sum(jnp.where(row == col, lower_c, 0.0), axis=0)
    payload = jnp.concatenate([folded, block_b], axis=1)
    extra = jnp.concatenate([diag_c, jnp.zeros((h,), jnp.float32)])[None, :]
    rows = -(-(h + 1) // size) * size
    payload = jnp.concatenate(
        [payload, extra, jnp.zeros((rows - h - 1, 2 * h), jnp.float32)], axis=0
    )
    per = rows // size
    blocks = payload.reshape(size, per, 2 * h)
    me = lax.axis_index(axis)
    acc = lax.dynamic_index_in_dim(blocks, me, 0, keepdims=False)
    for s in range(1, size):
        outgoing = lax.dynamic_index_in_dim(blocks, (me + s) % size, 0, keepdims=False)
        acc = acc + lax.ppermute(outgoing, axis, _shift_pairs(size, s))
    mine = acc.astype(jnp.bfloat16)
    spread = jnp.broadcast_to(mine[None], (size,) + mine.shape)
    full = lax.all_to_all(spread, axis, split_axis=0, concat_axis=0, tiled=True).reshape(rows, 2 * h)
    folded_r = full[:h, :h]
    block_br = full[:h, h:]
    diag_cr = full[h, :h]
    upper_r = jnp.where(row <= col, folded_r, folded_r.T)
    lower_r = jnp.where(row > col, folded_r, folded_r.T)
    lower_r = jnp.where(row == col, diag_cr[None, :], lower_r)
    top = jnp.concatenate([upper_r, block_br], axis=1)
    bottom = jnp.concatenate([block_br.T, lower_r], axis=1)
    return jnp.concatenate([top, bottom], axis=0)


def gather_slots(mine, axis, size):
    if size & (size - 1) != 0:
        full = lax.all_gather(mine[None], axis, axis=0, tiled=True)
        me = lax.axis_index(axis)
        return jnp.take(full, jnp.arange(size, dtype=jnp.int32) ^ me, axis=0, mode="clip")
    return gather_slots_from({0: mine}, axis, size, size // 2)


def gather_slots_from(held, axis, size, bit):
    held = dict(held)
    while bit >= 1:
        keys = sorted(held)
        sent = jnp.stack([held[j] for j in keys])
        got = lax.ppermute(sent, axis, [(i, i ^ bit) for i in range(size)])
        for n, j in enumerate(keys):
            held[j ^ bit] = got[n]
        bit //= 2
    return jnp.stack([held[j] for j in range(size)])


def per_device(grad, momentum, owner):
    size = lax.axis_size("tensor")
    new_momentum = decay * momentum + grad.astype(jnp.float32)
    direction = grad.astype(jnp.float32) + decay * new_momentum
    total = total_over(jnp.sum(direction * direction), "tensor", size)
    rows_here = (direction[0] / (jnp.sqrt(total) + eps)).astype(jnp.bfloat16)
    columns = lax.all_to_all(rows_here, "tensor", split_axis=1, concat_axis=0, tiled=True)
    for step in range(ITERS):
        partial = jnp.dot(columns, columns.T, preferred_element_type=jnp.float32)
        gram = gram_allreduce(partial, "tensor", size)
        square = jnp.dot(gram, gram, preferred_element_type=jnp.float32)
        poly = (coef_b * gram.astype(jnp.float32) + coef_c * square).astype(jnp.bfloat16)
        applied = jnp.dot(poly, columns, preferred_element_type=jnp.float32)
        columns = (coef_a * columns.astype(jnp.float32) + applied).astype(jnp.bfloat16)
    factor = 0.2 * math.sqrt(max(M, N))
    per = columns.shape[0] // size
    half = min(per, 8 * ((per * 2 + 12) // 24))
    blocks = columns.reshape(size, per, columns.shape[1])
    slots = lax.axis_size("dp")
    ids = jnp.arange(slots, dtype=jnp.int32)
    inverse = jnp.sum(
        jnp.where(owner[None, :] == ids[:, None], ids[None, :], 0), axis=1
    )
    where_from = inverse ^ lax.axis_index("dp")
    cut = half if half < per else per
    hb = slots // 2
    pieces = []
    first = blocks[:, :cut, :].reshape(size * cut, columns.shape[1])
    if cut < per and slots > 1 and slots & (slots - 1) == 0:
        late = blocks[:, cut:, :]
        partner = lax.ppermute(late, "dp", [(i, i ^ hb) for i in range(slots)])
    back_rows = lax.all_to_all(first, "tensor", split_axis=0, concat_axis=1, tiled=True)
    scaled = (factor * back_rows.astype(jnp.float32)).astype(jnp.bfloat16)
    if cut < per and slots > 1 and slots & (slots - 1) == 0:
        both = jnp.stack([late, partner], axis=1).reshape(size * 2 * (per - cut), columns.shape[1])
        both, scaled = lax.optimization_barrier((both, scaled))
    pieces.append(gather_slots(scaled, "dp", slots))
    if cut < per and slots > 1 and slots & (slots - 1) == 0:
        back_rows = lax.all_to_all(both, "tensor", split_axis=0, concat_axis=1, tiled=True)
        scaled = (factor * back_rows.astype(jnp.float32)).astype(jnp.bfloat16)
        scaled = scaled.reshape(2, per - cut, scaled.shape[1])
        pieces.append(gather_slots_from({0: scaled[0], hb: scaled[1]}, "dp", slots, hb // 2))
    elif cut < per:
        rest = blocks[:, cut:, :].reshape(size * (per - cut), columns.shape[1])
        back_rows = lax.all_to_all(rest, "tensor", split_axis=0, concat_axis=1, tiled=True)
        scaled = (factor * back_rows.astype(jnp.float32)).astype(jnp.bfloat16)
        pieces.append(gather_slots(scaled, "dp", slots))
    rows = []
    for m in range(slots):
        rows.append(
            jnp.concatenate(
                [lax.dynamic_index_in_dim(p, where_from[m], 0, keepdims=True) for p in pieces],
                axis=1,
            )
        )
    update = jnp.concatenate(rows, axis=0)
    return (update, new_momentum)


def solution(mesh):
    in_specs = (P("dp", "tensor", None), P("dp", "tensor", None), P())
    out_specs = (P(None, "tensor", None), P("dp", "tensor", None))
    return jax.shard_map(
        per_device, mesh=mesh, in_specs=in_specs, out_specs=out_specs, check_vma=False
    )
```

```python
import math

import jax
import jax.numpy as jnp
from jax import lax
from jax.sharding import PartitionSpec as P

M = 576
N = 6144
ITERS = 2


coef_a = 3.4445
coef_b = -4.775
coef_c = 2.0315
decay = 0.95
eps = 1e-07


def _shift_pairs(size, s):
    return [(i, (i + s) % size) for i in range(size)]


def total_over(value, axis, size):
    spread = jnp.broadcast_to(value, (size, 1))
    got = lax.all_to_all(spread, axis, split_axis=0, concat_axis=0, tiled=True)
    return jnp.sum(got)


def gram_allreduce(partial, axis, size):
    n = partial.shape[0]
    h = n // 2
    upper_a = partial[:h, :h]
    block_b = partial[:h, h:]
    lower_c = partial[h:, h:]
    row = lax.broadcasted_iota(jnp.int32, (h, h), 0)
    col = lax.broadcasted_iota(jnp.int32, (h, h), 1)
    folded = jnp.where(row <= col, upper_a, lower_c)
    diag_c = jnp.sum(jnp.where(row == col, lower_c, 0.0), axis=0)
    payload = jnp.concatenate([folded, block_b], axis=1)
    extra = jnp.concatenate([diag_c, jnp.zeros((h,), jnp.float32)])[None, :]
    rows = -(-(h + 1) // size) * size
    payload = jnp.concatenate(
        [payload, extra, jnp.zeros((rows - h - 1, 2 * h), jnp.float32)], axis=0
    )
    per = rows // size
    blocks = payload.reshape(size, per, 2 * h)
    me = lax.axis_index(axis)
    acc = lax.dynamic_index_in_dim(blocks, me, 0, keepdims=False)
    for s in range(1, size):
        outgoing = lax.dynamic_index_in_dim(blocks, (me + s) % size, 0, keepdims=False)
        acc = acc + lax.ppermute(outgoing, axis, _shift_pairs(size, s))
    mine = acc.astype(jnp.bfloat16)
    if size & (size - 1) == 0:
        relative = gather_slots(mine, axis, size)
        order = jnp.arange(size, dtype=jnp.int32) ^ me
        full = jnp.take(relative, order, axis=0, mode="clip").reshape(rows, 2 * h)
    else:
        spread = jnp.broadcast_to(mine[None], (size,) + mine.shape)
        full = lax.all_to_all(spread, axis, split_axis=0, concat_axis=0, tiled=True).reshape(rows, 2 * h)
    folded_r = full[:h, :h]
    block_br = full[:h, h:]
    diag_cr = full[h, :h]
    upper_r = jnp.where(row <= col, folded_r, folded_r.T)
    lower_r = jnp.where(row > col, folded_r, folded_r.T)
    lower_r = jnp.where(row == col, diag_cr[None, :], lower_r)
    top = jnp.concatenate([upper_r, block_br], axis=1)
    bottom = jnp.concatenate([block_br.T, lower_r], axis=1)
    return jnp.concatenate([top, bottom], axis=0)


def gather_slots(mine, axis, size):
    if size & (size - 1) != 0:
        full = lax.all_gather(mine[None], axis, axis=0, tiled=True)
        me = lax.axis_index(axis)
        return jnp.take(full, jnp.arange(size, dtype=jnp.int32) ^ me, axis=0, mode="clip")
    held = {0: mine}
    bit = size // 2
    while bit >= 1:
        keys = sorted(held)
        sent = jnp.stack([held[j] for j in keys])
        got = lax.ppermute(sent, axis, [(i, i ^ bit) for i in range(size)])
        for n, j in enumerate(keys):
            held[j ^ bit] = got[n]
        bit //= 2
    return jnp.stack([held[j] for j in range(size)])


def per_device(grad, momentum, owner):
    size = lax.axis_size("tensor")
    new_momentum = decay * momentum + grad.astype(jnp.float32)
    direction = grad.astype(jnp.float32) + decay * new_momentum
    total = total_over(jnp.sum(direction * direction), "tensor", size)
    rows_here = (direction[0] / (jnp.sqrt(total) + eps)).astype(jnp.bfloat16)
    columns = lax.all_to_all(rows_here, "tensor", split_axis=1, concat_axis=0, tiled=True)
    for step in range(ITERS):
        partial = jnp.dot(columns, columns.T, preferred_element_type=jnp.float32)
        gram = gram_allreduce(partial, "tensor", size)
        square = jnp.dot(gram, gram, preferred_element_type=jnp.float32)
        poly = (coef_b * gram.astype(jnp.float32) + coef_c * square).astype(jnp.bfloat16)
        applied = jnp.dot(poly, columns, preferred_element_type=jnp.float32)
        columns = (coef_a * columns.astype(jnp.float32) + applied).astype(jnp.bfloat16)
    factor = 0.2 * math.sqrt(max(M, N))
    per = columns.shape[0] // size
    half = min(per, 8 * ((per * 9 + 64) // 128))
    blocks = columns.reshape(size, per, columns.shape[1])
    slots = lax.axis_size("dp")
    ids = jnp.arange(slots, dtype=jnp.int32)
    inverse = jnp.sum(
        jnp.where(owner[None, :] == ids[:, None], ids[None, :], 0), axis=1
    )
    where_from = inverse ^ lax.axis_index("dp")
    bounds = ((0, half), (half, per)) if half < per else ((0, per),)
    parts = [
        blocks[:, lo:hi, :].reshape(size * (hi - lo), columns.shape[1]) for lo, hi in bounds
    ]
    pieces = []
    for n in range(len(parts)):
        back_rows = lax.all_to_all(parts[n], "tensor", split_axis=0, concat_axis=1, tiled=True)
        if n + 1 < len(parts):
            parts[n + 1], back_rows = lax.optimization_barrier((parts[n + 1], back_rows))
        scaled = (factor * back_rows.astype(jnp.float32)).astype(jnp.bfloat16)
        pieces.append(gather_slots(scaled, "dp", slots))
    rows = []
    for m in range(slots):
        rows.append(
            jnp.concatenate(
                [lax.dynamic_index_in_dim(p, where_from[m], 0, keepdims=True) for p in pieces],
                axis=1,
            )
        )
    update = jnp.concatenate(rows, axis=0)
    return (update, new_momentum)


def solution(mesh):
    in_specs = (P("dp", "tensor", None), P("dp", "tensor", None), P())
    out_specs = (P(None, "tensor", None), P("dp", "tensor", None))
    return jax.shard_map(
        per_device, mesh=mesh, in_specs=in_specs, out_specs=out_specs, check_vma=False
    )
```

```python
import math

import jax
import jax.numpy as jnp
from jax import lax
from jax.sharding import PartitionSpec as P

M = 576
N = 6144
ITERS = 2


coef_a = 3.4445
coef_b = -4.775
coef_c = 2.0315
decay = 0.95
eps = 1e-07


def _shift_pairs(size, s):
    return [(i, (i + s) % size) for i in range(size)]


def total_over(value, axis, size):
    spread = jnp.broadcast_to(value, (size, 1))
    got = lax.all_to_all(spread, axis, split_axis=0, concat_axis=0, tiled=True)
    return jnp.sum(got)


def gram_allreduce(partial, axis, size):
    n = partial.shape[0]
    h = n // 2
    upper_a = partial[:h, :h]
    block_b = partial[:h, h:]
    lower_c = partial[h:, h:]
    row = lax.broadcasted_iota(jnp.int32, (h, h), 0)
    col = lax.broadcasted_iota(jnp.int32, (h, h), 1)
    folded = jnp.where(row <= col, upper_a, lower_c)
    diag_c = jnp.sum(jnp.where(row == col, lower_c, 0.0), axis=0)
    payload = jnp.concatenate([folded, block_b], axis=1)
    extra = jnp.concatenate([diag_c, jnp.zeros((h,), jnp.float32)])[None, :]
    rows = -(-(h + 1) // size) * size
    payload = jnp.concatenate(
        [payload, extra, jnp.zeros((rows - h - 1, 2 * h), jnp.float32)], axis=0
    )
    per = rows // size
    blocks = payload.reshape(size, per, 2 * h)
    me = lax.axis_index(axis)
    if size & (size - 1) == 0:
        relative = jnp.take(blocks, jnp.arange(size, dtype=jnp.int32) ^ me, axis=0, mode="clip")
        cur = {r: relative[r] for r in range(size)}
        bit = 1
        while bit < size:
            send_keys = [r for r in sorted(cur) if r & bit]
            got = lax.ppermute(
                jnp.stack([cur[r] for r in send_keys]), axis, [(i, i ^ bit) for i in range(size)]
            )
            cur = {r ^ bit: cur[r ^ bit] + got[n] for n, r in enumerate(send_keys)}
            bit *= 2
        acc = cur[0]
    else:
        acc = lax.dynamic_index_in_dim(blocks, me, 0, keepdims=False)
        for s in range(1, size):
            outgoing = lax.dynamic_index_in_dim(blocks, (me + s) % size, 0, keepdims=False)
            acc = acc + lax.ppermute(outgoing, axis, _shift_pairs(size, s))
    mine = acc.astype(jnp.bfloat16)
    if size & (size - 1) == 0:
        relative = gather_slots(mine, axis, size)
        order = jnp.arange(size, dtype=jnp.int32) ^ me
        full = jnp.take(relative, order, axis=0, mode="clip").reshape(rows, 2 * h)
    else:
        spread = jnp.broadcast_to(mine[None], (size,) + mine.shape)
        full = lax.all_to_all(spread, axis, split_axis=0, concat_axis=0, tiled=True).reshape(rows, 2 * h)
    folded_r = full[:h, :h]
    block_br = full[:h, h:]
    diag_cr = full[h, :h]
    upper_r = jnp.where(row <= col, folded_r, folded_r.T)
    lower_r = jnp.where(row > col, folded_r, folded_r.T)
    lower_r = jnp.where(row == col, diag_cr[None, :], lower_r)
    top = jnp.concatenate([upper_r, block_br], axis=1)
    bottom = jnp.concatenate([block_br.T, lower_r], axis=1)
    return jnp.concatenate([top, bottom], axis=0)


def gather_slots(mine, axis, size):
    if size & (size - 1) != 0:
        full = lax.all_gather(mine[None], axis, axis=0, tiled=True)
        me = lax.axis_index(axis)
        return jnp.take(full, jnp.arange(size, dtype=jnp.int32) ^ me, axis=0, mode="clip")
    held = {0: mine}
    bit = size // 2
    while bit >= 1:
        keys = sorted(held)
        sent = jnp.stack([held[j] for j in keys])
        got = lax.ppermute(sent, axis, [(i, i ^ bit) for i in range(size)])
        for n, j in enumerate(keys):
            held[j ^ bit] = got[n]
        bit //= 2
    return jnp.stack([held[j] for j in range(size)])


def per_device(grad, momentum, owner):
    size = lax.axis_size("tensor")
    new_momentum = decay * momentum + grad.astype(jnp.float32)
    direction = grad.astype(jnp.float32) + decay * new_momentum
    total = total_over(jnp.sum(direction * direction), "tensor", size)
    rows_here = (direction[0] / (jnp.sqrt(total) + eps)).astype(jnp.bfloat16)
    columns = lax.all_to_all(rows_here, "tensor", split_axis=1, concat_axis=0, tiled=True)
    for step in range(ITERS):
        partial = jnp.dot(columns, columns.T, preferred_element_type=jnp.float32)
        gram = gram_allreduce(partial, "tensor", size)
        square = jnp.dot(gram, gram, preferred_element_type=jnp.float32)
        poly = (coef_b * gram.astype(jnp.float32) + coef_c * square).astype(jnp.bfloat16)
        applied = jnp.dot(poly, columns, preferred_element_type=jnp.float32)
        columns = (coef_a * columns.astype(jnp.float32) + applied).astype(jnp.bfloat16)
    factor = 0.2 * math.sqrt(max(M, N))
    per = columns.shape[0] // size
    half = min(per, 8 * ((per * 9 + 64) // 128))
    blocks = columns.reshape(size, per, columns.shape[1])
    slots = lax.axis_size("dp")
    ids = jnp.arange(slots, dtype=jnp.int32)
    inverse = jnp.sum(
        jnp.where(owner[None, :] == ids[:, None], ids[None, :], 0), axis=1
    )
    where_from = inverse ^ lax.axis_index("dp")
    bounds = ((0, half), (half, per)) if half < per else ((0, per),)
    parts = [
        blocks[:, lo:hi, :].reshape(size * (hi - lo), columns.shape[1]) for lo, hi in bounds
    ]
    pieces = []
    for n in range(len(parts)):
        back_rows = lax.all_to_all(parts[n], "tensor", split_axis=0, concat_axis=1, tiled=True)
        if n + 1 < len(parts):
            parts[n + 1], back_rows = lax.optimization_barrier((parts[n + 1], back_rows))
        scaled = (factor * back_rows.astype(jnp.float32)).astype(jnp.bfloat16)
        pieces.append(gather_slots(scaled, "dp", slots))
    rows = []
    for m in range(slots):
        rows.append(
            jnp.concatenate(
                [lax.dynamic_index_in_dim(p, where_from[m], 0, keepdims=True) for p in pieces],
                axis=1,
            )
        )
    update = jnp.concatenate(rows, axis=0)
    return (update, new_momentum)


def solution(mesh):
    in_specs = (P("dp", "tensor", None), P("dp", "tensor", None), P())
    out_specs = (P(None, "tensor", None), P("dp", "tensor", None))
    return jax.shard_map(
        per_device, mesh=mesh, in_specs=in_specs, out_specs=out_specs, check_vma=False
    )
```

```python
import math

import jax
import jax.numpy as jnp
from jax import lax
from jax.sharding import PartitionSpec as P

M = 576
N = 6144
ITERS = 2


coef_a = 3.4445
coef_b = -4.775
coef_c = 2.0315
decay = 0.95
eps = 1e-07


def _shift_pairs(size, s):
    return [(i, (i + s) % size) for i in range(size)]


def total_over(value, axis, size):
    spread = jnp.broadcast_to(value, (size, 1))
    got = lax.all_to_all(spread, axis, split_axis=0, concat_axis=0, tiled=True)
    return jnp.sum(got)


def gram_allreduce(partial, axis, size):
    n = partial.shape[0]
    h = n // 2
    upper_a = partial[:h, :h]
    block_b = partial[:h, h:]
    lower_c = partial[h:, h:]
    row = lax.broadcasted_iota(jnp.int32, (h, h), 0)
    col = lax.broadcasted_iota(jnp.int32, (h, h), 1)
    folded = jnp.where(row <= col, upper_a, lower_c)
    diag_c = jnp.sum(jnp.where(row == col, lower_c, 0.0), axis=0)
    payload = jnp.concatenate([folded, block_b], axis=1)
    extra = jnp.concatenate([diag_c, jnp.zeros((h,), jnp.float32)])[None, :]
    rows = -(-(h + 1) // size) * size
    payload = jnp.concatenate(
        [payload, extra, jnp.zeros((rows - h - 1, 2 * h), jnp.float32)], axis=0
    )
    per = rows // size
    blocks = payload.reshape(size, per, 2 * h)
    me = lax.axis_index(axis)
    acc = lax.dynamic_index_in_dim(blocks, me, 0, keepdims=False)
    for s in range(1, size):
        if size & (size - 1) == 0:
            target, pairs = me ^ s, [(i, i ^ s) for i in range(size)]
        else:
            target, pairs = (me + s) % size, _shift_pairs(size, s)
        outgoing = lax.dynamic_index_in_dim(blocks, target, 0, keepdims=False)
        acc = acc + lax.ppermute(outgoing, axis, pairs)
    mine = acc.astype(jnp.bfloat16)
    if size & (size - 1) == 0:
        relative = gather_slots(mine, axis, size)
        order = jnp.arange(size, dtype=jnp.int32) ^ me
        full = jnp.take(relative, order, axis=0, mode="clip").reshape(rows, 2 * h)
    else:
        spread = jnp.broadcast_to(mine[None], (size,) + mine.shape)
        full = lax.all_to_all(spread, axis, split_axis=0, concat_axis=0, tiled=True).reshape(rows, 2 * h)
    folded_r = full[:h, :h]
    block_br = full[:h, h:]
    diag_cr = full[h, :h]
    upper_r = jnp.where(row <= col, folded_r, folded_r.T)
    lower_r = jnp.where(row > col, folded_r, folded_r.T)
    lower_r = jnp.where(row == col, diag_cr[None, :], lower_r)
    top = jnp.concatenate([upper_r, block_br], axis=1)
    bottom = jnp.concatenate([block_br.T, lower_r], axis=1)
    return jnp.concatenate([top, bottom], axis=0)


def gather_slots(mine, axis, size):
    if size & (size - 1) != 0:
        full = lax.all_gather(mine[None], axis, axis=0, tiled=True)
        me = lax.axis_index(axis)
        return jnp.take(full, jnp.arange(size, dtype=jnp.int32) ^ me, axis=0, mode="clip")
    held = {0: mine}
    bit = size // 2
    while bit >= 1:
        keys = sorted(held)
        sent = jnp.stack([held[j] for j in keys])
        got = lax.ppermute(sent, axis, [(i, i ^ bit) for i in range(size)])
        for n, j in enumerate(keys):
            held[j ^ bit] = got[n]
        bit //= 2
    return jnp.stack([held[j] for j in range(size)])


def per_device(grad, momentum, owner):
    size = lax.axis_size("tensor")
    new_momentum = decay * momentum + grad.astype(jnp.float32)
    direction = grad.astype(jnp.float32) + decay * new_momentum
    total = total_over(jnp.sum(direction * direction), "tensor", size)
    rows_here = (direction[0] / (jnp.sqrt(total) + eps)).astype(jnp.bfloat16)
    columns = lax.all_to_all(rows_here, "tensor", split_axis=1, concat_axis=0, tiled=True)
    for step in range(ITERS):
        partial = jnp.dot(columns, columns.T, preferred_element_type=jnp.float32)
        gram = gram_allreduce(partial, "tensor", size)
        square = jnp.dot(gram, gram, preferred_element_type=jnp.float32)
        poly = (coef_b * gram.astype(jnp.float32) + coef_c * square).astype(jnp.bfloat16)
        applied = jnp.dot(poly, columns, preferred_element_type=jnp.float32)
        columns = (coef_a * columns.astype(jnp.float32) + applied).astype(jnp.bfloat16)
    factor = 0.2 * math.sqrt(max(M, N))
    per = columns.shape[0] // size
    half = min(per, 8 * ((per * 9 + 64) // 128))
    blocks = columns.reshape(size, per, columns.shape[1])
    slots = lax.axis_size("dp")
    ids = jnp.arange(slots, dtype=jnp.int32)
    inverse = jnp.sum(
        jnp.where(owner[None, :] == ids[:, None], ids[None, :], 0), axis=1
    )
    where_from = inverse ^ lax.axis_index("dp")
    bounds = ((0, half), (half, per)) if half < per else ((0, per),)
    parts = [
        blocks[:, lo:hi, :].reshape(size * (hi - lo), columns.shape[1]) for lo, hi in bounds
    ]
    pieces = []
    for n in range(len(parts)):
        back_rows = lax.all_to_all(parts[n], "tensor", split_axis=0, concat_axis=1, tiled=True)
        if n + 1 < len(parts):
            parts[n + 1], back_rows = lax.optimization_barrier((parts[n + 1], back_rows))
        scaled = (factor * back_rows.astype(jnp.float32)).astype(jnp.bfloat16)
        pieces.append(gather_slots(scaled, "dp", slots))
    rows = []
    for m in range(slots):
        rows.append(
            jnp.concatenate(
                [lax.dynamic_index_in_dim(p, where_from[m], 0, keepdims=True) for p in pieces],
                axis=1,
            )
        )
    update = jnp.concatenate(rows, axis=0)
    return (update, new_momentum)


def solution(mesh):
    in_specs = (P("dp", "tensor", None), P("dp", "tensor", None), P())
    out_specs = (P(None, "tensor", None), P("dp", "tensor", None))
    return jax.shard_map(
        per_device, mesh=mesh, in_specs=in_specs, out_specs=out_specs, check_vma=False
    )
```

```python
import math

import jax
import jax.numpy as jnp
from jax import lax
from jax.sharding import PartitionSpec as P

M = 576
N = 6144
ITERS = 2


coef_a = 3.4445
coef_b = -4.775
coef_c = 2.0315
decay = 0.95
eps = 1e-07


def _shift_pairs(size, s):
    return [(i, (i + s) % size) for i in range(size)]


def total_over(value, axis, size):
    spread = jnp.broadcast_to(value, (size, 1))
    got = lax.all_to_all(spread, axis, split_axis=0, concat_axis=0, tiled=True)
    return jnp.sum(got)


def gram_allreduce(partial, axis, size):
    n = partial.shape[0]
    h = n // 2
    upper_a = partial[:h, :h]
    block_b = partial[:h, h:]
    lower_c = partial[h:, h:]
    row = lax.broadcasted_iota(jnp.int32, (h, h), 0)
    col = lax.broadcasted_iota(jnp.int32, (h, h), 1)
    folded = jnp.where(row <= col, upper_a, lower_c)
    diag_c = jnp.sum(jnp.where(row == col, lower_c, 0.0), axis=0)
    payload = jnp.concatenate([folded, block_b], axis=1)
    extra = jnp.concatenate([diag_c, jnp.zeros((h,), jnp.float32)])[None, :]
    rows = -(-(h + 1) // size) * size
    payload = jnp.concatenate(
        [payload, extra, jnp.zeros((rows - h - 1, 2 * h), jnp.float32)], axis=0
    )
    per = rows // size
    blocks = payload.reshape(size, per, 2 * h)
    me = lax.axis_index(axis)
    acc = lax.dynamic_index_in_dim(blocks, me, 0, keepdims=False)
    for s in range(1, size):
        if size & (size - 1) == 0:
            target, pairs = me ^ s, [(i, i ^ s) for i in range(size)]
        else:
            target, pairs = (me + s) % size, _shift_pairs(size, s)
        outgoing = lax.dynamic_index_in_dim(blocks, target, 0, keepdims=False)
        acc = acc + lax.ppermute(outgoing, axis, pairs)
    mine = acc.astype(jnp.bfloat16)
    if size & (size - 1) == 0:
        relative = gather_slots(mine, axis, size)
        order = jnp.arange(size, dtype=jnp.int32) ^ me
        full = jnp.take(relative, order, axis=0, mode="clip").reshape(rows, 2 * h)
    else:
        spread = jnp.broadcast_to(mine[None], (size,) + mine.shape)
        full = lax.all_to_all(spread, axis, split_axis=0, concat_axis=0, tiled=True).reshape(rows, 2 * h)
    folded_r = full[:h, :h]
    block_br = full[:h, h:]
    diag_cr = full[h, :h]
    upper_r = jnp.where(row <= col, folded_r, folded_r.T)
    lower_r = jnp.where(row > col, folded_r, folded_r.T)
    lower_r = jnp.where(row == col, diag_cr[None, :], lower_r)
    top = jnp.concatenate([upper_r, block_br], axis=1)
    bottom = jnp.concatenate([block_br.T, lower_r], axis=1)
    return jnp.concatenate([top, bottom], axis=0)


def gather_slots(mine, axis, size):
    if size & (size - 1) != 0:
        full = lax.all_gather(mine[None], axis, axis=0, tiled=True)
        me = lax.axis_index(axis)
        return jnp.take(full, jnp.arange(size, dtype=jnp.int32) ^ me, axis=0, mode="clip")
    held = {0: mine}
    bit = size // 2
    while bit >= 1:
        keys = sorted(held)
        sent = jnp.stack([held[j] for j in keys])
        got = lax.ppermute(sent, axis, [(i, i ^ bit) for i in range(size)])
        for n, j in enumerate(keys):
            held[j ^ bit] = got[n]
        bit //= 2
    return jnp.stack([held[j] for j in range(size)])


def per_device(grad, momentum, owner):
    size = lax.axis_size("tensor")
    new_momentum = decay * momentum + grad.astype(jnp.float32)
    direction = grad.astype(jnp.float32) + decay * new_momentum
    total = total_over(jnp.sum(direction * direction), "tensor", size)
    rows_here = (direction[0] / (jnp.sqrt(total) + eps)).astype(jnp.bfloat16)
    if size & (size - 1) == 0:
        me = lax.axis_index("tensor")
        width = rows_here.shape[1] // size
        by_col = rows_here.reshape(rows_here.shape[0], size, width)
        got = [lax.dynamic_index_in_dim(by_col, me, 1, keepdims=False)]
        for k in range(1, size):
            outgoing = lax.dynamic_index_in_dim(by_col, me ^ k, 1, keepdims=False)
            got.append(lax.ppermute(outgoing, "tensor", [(i, i ^ k) for i in range(size)]))
        relative = jnp.stack(got)
        order = jnp.arange(size, dtype=jnp.int32) ^ me
        columns = jnp.take(relative, order, axis=0, mode="clip").reshape(size * rows_here.shape[0], width)
    else:
        columns = lax.all_to_all(rows_here, "tensor", split_axis=1, concat_axis=0, tiled=True)
    for step in range(ITERS):
        partial = jnp.dot(columns, columns.T, preferred_element_type=jnp.float32)
        gram = gram_allreduce(partial, "tensor", size)
        square = jnp.dot(gram, gram, preferred_element_type=jnp.float32)
        poly = (coef_b * gram.astype(jnp.float32) + coef_c * square).astype(jnp.bfloat16)
        applied = jnp.dot(poly, columns, preferred_element_type=jnp.float32)
        columns = (coef_a * columns.astype(jnp.float32) + applied).astype(jnp.bfloat16)
    factor = 0.2 * math.sqrt(max(M, N))
    per = columns.shape[0] // size
    half = min(per, 8 * ((per * 9 + 64) // 128))
    blocks = columns.reshape(size, per, columns.shape[1])
    slots = lax.axis_size("dp")
    ids = jnp.arange(slots, dtype=jnp.int32)
    inverse = jnp.sum(
        jnp.where(owner[None, :] == ids[:, None], ids[None, :], 0), axis=1
    )
    where_from = inverse ^ lax.axis_index("dp")
    bounds = ((0, half), (half, per)) if half < per else ((0, per),)
    parts = [
        blocks[:, lo:hi, :].reshape(size * (hi - lo), columns.shape[1]) for lo, hi in bounds
    ]
    pieces = []
    for n in range(len(parts)):
        back_rows = lax.all_to_all(parts[n], "tensor", split_axis=0, concat_axis=1, tiled=True)
        if n + 1 < len(parts):
            parts[n + 1], back_rows = lax.optimization_barrier((parts[n + 1], back_rows))
        scaled = (factor * back_rows.astype(jnp.float32)).astype(jnp.bfloat16)
        pieces.append(gather_slots(scaled, "dp", slots))
    rows = []
    for m in range(slots):
        rows.append(
            jnp.concatenate(
                [lax.dynamic_index_in_dim(p, where_from[m], 0, keepdims=True) for p in pieces],
                axis=1,
            )
        )
    update = jnp.concatenate(rows, axis=0)
    return (update, new_momentum)


def solution(mesh):
    in_specs = (P("dp", "tensor", None), P("dp", "tensor", None), P())
    out_specs = (P(None, "tensor", None), P("dp", "tensor", None))
    return jax.shard_map(
        per_device, mesh=mesh, in_specs=in_specs, out_specs=out_specs, check_vma=False
    )
```

```python
import math

import jax
import jax.numpy as jnp
from jax import lax
from jax.sharding import PartitionSpec as P

M = 576
N = 6144
ITERS = 2


coef_a = 3.4445
coef_b = -4.775
coef_c = 2.0315
decay = 0.95
eps = 1e-07


def _shift_pairs(size, s):
    return [(i, (i + s) % size) for i in range(size)]


def total_over(value, axis, size):
    spread = jnp.broadcast_to(value, (size, 1))
    got = lax.all_to_all(spread, axis, split_axis=0, concat_axis=0, tiled=True)
    return jnp.sum(got)


def gram_allreduce(partial, axis, size):
    n = partial.shape[0]
    h = n // 2
    upper_a = partial[:h, :h]
    block_b = partial[:h, h:]
    lower_c = partial[h:, h:]
    row = lax.broadcasted_iota(jnp.int32, (h, h), 0)
    col = lax.broadcasted_iota(jnp.int32, (h, h), 1)
    folded = jnp.where(row <= col, upper_a, lower_c)
    diag_c = jnp.sum(jnp.where(row == col, lower_c, 0.0), axis=0)
    payload = jnp.concatenate([folded, block_b], axis=1)
    extra = jnp.concatenate([diag_c, jnp.zeros((h,), jnp.float32)])[None, :]
    rows = -(-(h + 1) // size) * size
    payload = jnp.concatenate(
        [payload, extra, jnp.zeros((rows - h - 1, 2 * h), jnp.float32)], axis=0
    )
    per = rows // size
    blocks = payload.reshape(size, per, 2 * h)
    me = lax.axis_index(axis)
    acc = lax.dynamic_index_in_dim(blocks, me, 0, keepdims=False)
    for s in range(1, size):
        if size & (size - 1) == 0:
            target, pairs = me ^ s, [(i, i ^ s) for i in range(size)]
        else:
            target, pairs = (me + s) % size, _shift_pairs(size, s)
        outgoing = lax.dynamic_index_in_dim(blocks, target, 0, keepdims=False)
        acc = acc + lax.ppermute(outgoing, axis, pairs)
    mine = acc.astype(jnp.bfloat16)
    if size & (size - 1) == 0:
        relative = gather_slots(mine, axis, size)
        order = jnp.arange(size, dtype=jnp.int32) ^ me
        full = jnp.take(relative, order, axis=0, mode="clip").reshape(rows, 2 * h)
    else:
        spread = jnp.broadcast_to(mine[None], (size,) + mine.shape)
        full = lax.all_to_all(spread, axis, split_axis=0, concat_axis=0, tiled=True).reshape(rows, 2 * h)
    folded_r = full[:h, :h]
    block_br = full[:h, h:]
    diag_cr = full[h, :h]
    upper_r = jnp.where(row <= col, folded_r, folded_r.T)
    lower_r = jnp.where(row > col, folded_r, folded_r.T)
    lower_r = jnp.where(row == col, diag_cr[None, :], lower_r)
    top = jnp.concatenate([upper_r, block_br], axis=1)
    bottom = jnp.concatenate([block_br.T, lower_r], axis=1)
    return jnp.concatenate([top, bottom], axis=0)


def gather_slots(mine, axis, size):
    if size & (size - 1) != 0:
        full = lax.all_gather(mine[None], axis, axis=0, tiled=True)
        me = lax.axis_index(axis)
        return jnp.take(full, jnp.arange(size, dtype=jnp.int32) ^ me, axis=0, mode="clip")
    held = {0: mine}
    bit = size // 2
    while bit >= 1:
        keys = sorted(held)
        sent = jnp.stack([held[j] for j in keys])
        got = lax.ppermute(sent, axis, [(i, i ^ bit) for i in range(size)])
        for n, j in enumerate(keys):
            held[j ^ bit] = got[n]
        bit //= 2
    return jnp.stack([held[j] for j in range(size)])


def rows_from_columns(piece, axis, size):
    if size & (size - 1) != 0:
        return lax.all_to_all(piece, axis, split_axis=0, concat_axis=1, tiled=True)
    me = lax.axis_index(axis)
    k = piece.shape[0] // size
    width = piece.shape[1]
    by_dest = piece.reshape(size, k, width)
    got = [lax.dynamic_index_in_dim(by_dest, me, 0, keepdims=False)]
    for j in range(1, size):
        outgoing = lax.dynamic_index_in_dim(by_dest, me ^ j, 0, keepdims=False)
        got.append(lax.ppermute(outgoing, axis, [(i, i ^ j) for i in range(size)]))
    order = jnp.arange(size, dtype=jnp.int32) ^ me
    ordered = jnp.take(jnp.stack(got), order, axis=0, mode="clip")
    return ordered.transpose(1, 0, 2).reshape(k, size * width)


def per_device(grad, momentum, owner):
    size = lax.axis_size("tensor")
    new_momentum = decay * momentum + grad.astype(jnp.float32)
    direction = grad.astype(jnp.float32) + decay * new_momentum
    total = total_over(jnp.sum(direction * direction), "tensor", size)
    rows_here = (direction[0] / (jnp.sqrt(total) + eps)).astype(jnp.bfloat16)
    if size & (size - 1) == 0:
        me = lax.axis_index("tensor")
        width = rows_here.shape[1] // size
        by_col = rows_here.reshape(rows_here.shape[0], size, width)
        got = [lax.dynamic_index_in_dim(by_col, me, 1, keepdims=False)]
        for k in range(1, size):
            outgoing = lax.dynamic_index_in_dim(by_col, me ^ k, 1, keepdims=False)
            got.append(lax.ppermute(outgoing, "tensor", [(i, i ^ k) for i in range(size)]))
        relative = jnp.stack(got)
        order = jnp.arange(size, dtype=jnp.int32) ^ me
        columns = jnp.take(relative, order, axis=0, mode="clip").reshape(size * rows_here.shape[0], width)
    else:
        columns = lax.all_to_all(rows_here, "tensor", split_axis=1, concat_axis=0, tiled=True)
    for step in range(ITERS):
        partial = jnp.dot(columns, columns.T, preferred_element_type=jnp.float32)
        gram = gram_allreduce(partial, "tensor", size)
        square = jnp.dot(gram, gram, preferred_element_type=jnp.float32)
        poly = (coef_b * gram.astype(jnp.float32) + coef_c * square).astype(jnp.bfloat16)
        applied = jnp.dot(poly, columns, preferred_element_type=jnp.float32)
        columns = (coef_a * columns.astype(jnp.float32) + applied).astype(jnp.bfloat16)
    factor = 0.2 * math.sqrt(max(M, N))
    per = columns.shape[0] // size
    half = min(per, 8 * ((per * 9 + 64) // 128))
    blocks = columns.reshape(size, per, columns.shape[1])
    slots = lax.axis_size("dp")
    ids = jnp.arange(slots, dtype=jnp.int32)
    inverse = jnp.sum(
        jnp.where(owner[None, :] == ids[:, None], ids[None, :], 0), axis=1
    )
    where_from = inverse ^ lax.axis_index("dp")
    bounds = ((0, half), (half, per)) if half < per else ((0, per),)
    parts = [
        blocks[:, lo:hi, :].reshape(size * (hi - lo), columns.shape[1]) for lo, hi in bounds
    ]
    pieces = []
    for n in range(len(parts)):
        back_rows = rows_from_columns(parts[n], "tensor", size)
        if n + 1 < len(parts):
            parts[n + 1], back_rows = lax.optimization_barrier((parts[n + 1], back_rows))
        scaled = (factor * back_rows.astype(jnp.float32)).astype(jnp.bfloat16)
        pieces.append(gather_slots(scaled, "dp", slots))
    rows = []
    for m in range(slots):
        rows.append(
            jnp.concatenate(
                [lax.dynamic_index_in_dim(p, where_from[m], 0, keepdims=True) for p in pieces],
                axis=1,
            )
        )
    update = jnp.concatenate(rows, axis=0)
    return (update, new_momentum)


def solution(mesh):
    in_specs = (P("dp", "tensor", None), P("dp", "tensor", None), P())
    out_specs = (P(None, "tensor", None), P("dp", "tensor", None))
    return jax.shard_map(
        per_device, mesh=mesh, in_specs=in_specs, out_specs=out_specs, check_vma=False
    )
```

```python
import math

import jax
import jax.numpy as jnp
from jax import lax
from jax.sharding import PartitionSpec as P

M = 576
N = 6144
ITERS = 2


coef_a = 3.4445
coef_b = -4.775
coef_c = 2.0315
decay = 0.95
eps = 1e-07


def _shift_pairs(size, s):
    return [(i, (i + s) % size) for i in range(size)]


def total_over(value, axis, size):
    if size & (size - 1) == 0:
        me = lax.axis_index(axis)
        got = [value] + [
            lax.ppermute(value, axis, [(i, i ^ k) for i in range(size)]) for k in range(1, size)
        ]
        order = jnp.arange(size, dtype=jnp.int32) ^ me
        return jnp.sum(jnp.take(jnp.stack(got), order, mode="clip"))
    spread = jnp.broadcast_to(value, (size, 1))
    got = lax.all_to_all(spread, axis, split_axis=0, concat_axis=0, tiled=True)
    return jnp.sum(got)


def gram_allreduce(partial, axis, size):
    n = partial.shape[0]
    h = n // 2
    upper_a = partial[:h, :h]
    block_b = partial[:h, h:]
    lower_c = partial[h:, h:]
    row = lax.broadcasted_iota(jnp.int32, (h, h), 0)
    col = lax.broadcasted_iota(jnp.int32, (h, h), 1)
    folded = jnp.where(row <= col, upper_a, lower_c)
    diag_c = jnp.sum(jnp.where(row == col, lower_c, 0.0), axis=0)
    payload = jnp.concatenate([folded, block_b], axis=1)
    extra = jnp.concatenate([diag_c, jnp.zeros((h,), jnp.float32)])[None, :]
    rows = -(-(h + 1) // size) * size
    payload = jnp.concatenate(
        [payload, extra, jnp.zeros((rows - h - 1, 2 * h), jnp.float32)], axis=0
    )
    per = rows // size
    blocks = payload.reshape(size, per, 2 * h)
    me = lax.axis_index(axis)
    acc = lax.dynamic_index_in_dim(blocks, me, 0, keepdims=False)
    for s in range(1, size):
        if size & (size - 1) == 0:
            target, pairs = me ^ s, [(i, i ^ s) for i in range(size)]
        else:
            target, pairs = (me + s) % size, _shift_pairs(size, s)
        outgoing = lax.dynamic_index_in_dim(blocks, target, 0, keepdims=False)
        acc = acc + lax.ppermute(outgoing, axis, pairs)
    mine = acc.astype(jnp.bfloat16)
    if size & (size - 1) == 0:
        relative = gather_slots(mine, axis, size)
        order = jnp.arange(size, dtype=jnp.int32) ^ me
        full = jnp.take(relative, order, axis=0, mode="clip").reshape(rows, 2 * h)
    else:
        spread = jnp.broadcast_to(mine[None], (size,) + mine.shape)
        full = lax.all_to_all(spread, axis, split_axis=0, concat_axis=0, tiled=True).reshape(rows, 2 * h)
    folded_r = full[:h, :h]
    block_br = full[:h, h:]
    diag_cr = full[h, :h]
    upper_r = jnp.where(row <= col, folded_r, folded_r.T)
    lower_r = jnp.where(row > col, folded_r, folded_r.T)
    lower_r = jnp.where(row == col, diag_cr[None, :], lower_r)
    top = jnp.concatenate([upper_r, block_br], axis=1)
    bottom = jnp.concatenate([block_br.T, lower_r], axis=1)
    return jnp.concatenate([top, bottom], axis=0)


def gather_slots(mine, axis, size):
    if size & (size - 1) != 0:
        full = lax.all_gather(mine[None], axis, axis=0, tiled=True)
        me = lax.axis_index(axis)
        return jnp.take(full, jnp.arange(size, dtype=jnp.int32) ^ me, axis=0, mode="clip")
    held = {0: mine}
    bit = size // 2
    while bit >= 1:
        keys = sorted(held)
        sent = jnp.stack([held[j] for j in keys])
        got = lax.ppermute(sent, axis, [(i, i ^ bit) for i in range(size)])
        for n, j in enumerate(keys):
            held[j ^ bit] = got[n]
        bit //= 2
    return jnp.stack([held[j] for j in range(size)])


def per_device(grad, momentum, owner):
    size = lax.axis_size("tensor")
    new_momentum = decay * momentum + grad.astype(jnp.float32)
    direction = grad.astype(jnp.float32) + decay * new_momentum
    total = total_over(jnp.sum(direction * direction), "tensor", size)
    rows_here = (direction[0] / (jnp.sqrt(total) + eps)).astype(jnp.bfloat16)
    if size & (size - 1) == 0:
        me = lax.axis_index("tensor")
        width = rows_here.shape[1] // size
        by_col = rows_here.reshape(rows_here.shape[0], size, width)
        got = [lax.dynamic_index_in_dim(by_col, me, 1, keepdims=False)]
        for k in range(1, size):
            outgoing = lax.dynamic_index_in_dim(by_col, me ^ k, 1, keepdims=False)
            got.append(lax.ppermute(outgoing, "tensor", [(i, i ^ k) for i in range(size)]))
        relative = jnp.stack(got)
        order = jnp.arange(size, dtype=jnp.int32) ^ me
        columns = jnp.take(relative, order, axis=0, mode="clip").reshape(size * rows_here.shape[0], width)
    else:
        columns = lax.all_to_all(rows_here, "tensor", split_axis=1, concat_axis=0, tiled=True)
    for step in range(ITERS):
        partial = jnp.dot(columns, columns.T, preferred_element_type=jnp.float32)
        gram = gram_allreduce(partial, "tensor", size)
        square = jnp.dot(gram, gram, preferred_element_type=jnp.float32)
        poly = (coef_b * gram.astype(jnp.float32) + coef_c * square).astype(jnp.bfloat16)
        applied = jnp.dot(poly, columns, preferred_element_type=jnp.float32)
        columns = (coef_a * columns.astype(jnp.float32) + applied).astype(jnp.bfloat16)
    factor = 0.2 * math.sqrt(max(M, N))
    per = columns.shape[0] // size
    half = min(per, 8 * ((per * 9 + 64) // 128))
    blocks = columns.reshape(size, per, columns.shape[1])
    slots = lax.axis_size("dp")
    ids = jnp.arange(slots, dtype=jnp.int32)
    inverse = jnp.sum(
        jnp.where(owner[None, :] == ids[:, None], ids[None, :], 0), axis=1
    )
    where_from = inverse ^ lax.axis_index("dp")
    bounds = ((0, half), (half, per)) if half < per else ((0, per),)
    parts = [
        blocks[:, lo:hi, :].reshape(size * (hi - lo), columns.shape[1]) for lo, hi in bounds
    ]
    pieces = []
    for n in range(len(parts)):
        back_rows = lax.all_to_all(parts[n], "tensor", split_axis=0, concat_axis=1, tiled=True)
        if n + 1 < len(parts):
            parts[n + 1], back_rows = lax.optimization_barrier((parts[n + 1], back_rows))
        scaled = (factor * back_rows.astype(jnp.float32)).astype(jnp.bfloat16)
        pieces.append(gather_slots(scaled, "dp", slots))
    rows = []
    for m in range(slots):
        rows.append(
            jnp.concatenate(
                [lax.dynamic_index_in_dim(p, where_from[m], 0, keepdims=True) for p in pieces],
                axis=1,
            )
        )
    update = jnp.concatenate(rows, axis=0)
    return (update, new_momentum)


def solution(mesh):
    in_specs = (P("dp", "tensor", None), P("dp", "tensor", None), P())
    out_specs = (P(None, "tensor", None), P("dp", "tensor", None))
    return jax.shard_map(
        per_device, mesh=mesh, in_specs=in_specs, out_specs=out_specs, check_vma=False
    )
```

```python
import math

import jax
import jax.numpy as jnp
from jax import lax
from jax.sharding import PartitionSpec as P

M = 576
N = 6144
ITERS = 2


coef_a = 3.4445
coef_b = -4.775
coef_c = 2.0315
decay = 0.95
eps = 1e-07


def _shift_pairs(size, s):
    return [(i, (i + s) % size) for i in range(size)]


def total_over(value, axis, size):
    spread = jnp.broadcast_to(value, (size, 1))
    got = lax.all_to_all(spread, axis, split_axis=0, concat_axis=0, tiled=True)
    return jnp.sum(got)


def gram_allreduce(partial, axis, size):
    n = partial.shape[0]
    h = n // 2
    upper_a = partial[:h, :h]
    block_b = partial[:h, h:]
    lower_c = partial[h:, h:]
    row = lax.broadcasted_iota(jnp.int32, (h, h), 0)
    col = lax.broadcasted_iota(jnp.int32, (h, h), 1)
    folded = jnp.where(row <= col, upper_a, lower_c)
    diag_c = jnp.sum(jnp.where(row == col, lower_c, 0.0), axis=0)
    payload = jnp.concatenate([folded, block_b], axis=1)
    extra = jnp.concatenate([diag_c, jnp.zeros((h,), jnp.float32)])[None, :]
    rows = -(-(h + 1) // size) * size
    payload = jnp.concatenate(
        [payload, extra, jnp.zeros((rows - h - 1, 2 * h), jnp.float32)], axis=0
    )
    per = rows // size
    blocks = payload.reshape(size, per, 2 * h)
    me = lax.axis_index(axis)
    acc = lax.dynamic_index_in_dim(blocks, me, 0, keepdims=False)
    for s in range(1, size):
        if size & (size - 1) == 0:
            target, pairs = me ^ s, [(i, i ^ s) for i in range(size)]
        else:
            target, pairs = (me + s) % size, _shift_pairs(size, s)
        outgoing = lax.dynamic_index_in_dim(blocks, target, 0, keepdims=False)
        acc = acc + lax.ppermute(outgoing, axis, pairs)
    mine = acc.astype(jnp.bfloat16)
    if size & (size - 1) == 0:
        relative = jnp.stack(
            [mine] + [lax.ppermute(mine, axis, [(i, i ^ k) for i in range(size)]) for k in range(1, size)]
        )
        order = jnp.arange(size, dtype=jnp.int32) ^ me
        full = jnp.take(relative, order, axis=0, mode="clip").reshape(rows, 2 * h)
    else:
        spread = jnp.broadcast_to(mine[None], (size,) + mine.shape)
        full = lax.all_to_all(spread, axis, split_axis=0, concat_axis=0, tiled=True).reshape(rows, 2 * h)
    folded_r = full[:h, :h]
    block_br = full[:h, h:]
    diag_cr = full[h, :h]
    upper_r = jnp.where(row <= col, folded_r, folded_r.T)
    lower_r = jnp.where(row > col, folded_r, folded_r.T)
    lower_r = jnp.where(row == col, diag_cr[None, :], lower_r)
    top = jnp.concatenate([upper_r, block_br], axis=1)
    bottom = jnp.concatenate([block_br.T, lower_r], axis=1)
    return jnp.concatenate([top, bottom], axis=0)


def gather_slots(mine, axis, size):
    if size & (size - 1) != 0:
        full = lax.all_gather(mine[None], axis, axis=0, tiled=True)
        me = lax.axis_index(axis)
        return jnp.take(full, jnp.arange(size, dtype=jnp.int32) ^ me, axis=0, mode="clip")
    held = {0: mine}
    bit = size // 2
    while bit >= 1:
        keys = sorted(held)
        sent = jnp.stack([held[j] for j in keys])
        got = lax.ppermute(sent, axis, [(i, i ^ bit) for i in range(size)])
        for n, j in enumerate(keys):
            held[j ^ bit] = got[n]
        bit //= 2
    return jnp.stack([held[j] for j in range(size)])


def per_device(grad, momentum, owner):
    size = lax.axis_size("tensor")
    new_momentum = decay * momentum + grad.astype(jnp.float32)
    direction = grad.astype(jnp.float32) + decay * new_momentum
    total = total_over(jnp.sum(direction * direction), "tensor", size)
    rows_here = (direction[0] / (jnp.sqrt(total) + eps)).astype(jnp.bfloat16)
    if size & (size - 1) == 0:
        me = lax.axis_index("tensor")
        width = rows_here.shape[1] // size
        by_col = rows_here.reshape(rows_here.shape[0], size, width)
        got = [lax.dynamic_index_in_dim(by_col, me, 1, keepdims=False)]
        for k in range(1, size):
            outgoing = lax.dynamic_index_in_dim(by_col, me ^ k, 1, keepdims=False)
            got.append(lax.ppermute(outgoing, "tensor", [(i, i ^ k) for i in range(size)]))
        relative = jnp.stack(got)
        order = jnp.arange(size, dtype=jnp.int32) ^ me
        columns = jnp.take(relative, order, axis=0, mode="clip").reshape(size * rows_here.shape[0], width)
    else:
        columns = lax.all_to_all(rows_here, "tensor", split_axis=1, concat_axis=0, tiled=True)
    for step in range(ITERS):
        partial = jnp.dot(columns, columns.T, preferred_element_type=jnp.float32)
        gram = gram_allreduce(partial, "tensor", size)
        square = jnp.dot(gram, gram, preferred_element_type=jnp.float32)
        poly = (coef_b * gram.astype(jnp.float32) + coef_c * square).astype(jnp.bfloat16)
        applied = jnp.dot(poly, columns, preferred_element_type=jnp.float32)
        columns = (coef_a * columns.astype(jnp.float32) + applied).astype(jnp.bfloat16)
    factor = 0.2 * math.sqrt(max(M, N))
    per = columns.shape[0] // size
    half = min(per, 8 * ((per * 9 + 64) // 128))
    blocks = columns.reshape(size, per, columns.shape[1])
    slots = lax.axis_size("dp")
    ids = jnp.arange(slots, dtype=jnp.int32)
    inverse = jnp.sum(
        jnp.where(owner[None, :] == ids[:, None], ids[None, :], 0), axis=1
    )
    where_from = inverse ^ lax.axis_index("dp")
    bounds = ((0, half), (half, per)) if half < per else ((0, per),)
    parts = [
        blocks[:, lo:hi, :].reshape(size * (hi - lo), columns.shape[1]) for lo, hi in bounds
    ]
    pieces = []
    for n in range(len(parts)):
        back_rows = lax.all_to_all(parts[n], "tensor", split_axis=0, concat_axis=1, tiled=True)
        if n + 1 < len(parts):
            parts[n + 1], back_rows = lax.optimization_barrier((parts[n + 1], back_rows))
        scaled = (factor * back_rows.astype(jnp.float32)).astype(jnp.bfloat16)
        pieces.append(gather_slots(scaled, "dp", slots))
    rows = []
    for m in range(slots):
        rows.append(
            jnp.concatenate(
                [lax.dynamic_index_in_dim(p, where_from[m], 0, keepdims=True) for p in pieces],
                axis=1,
            )
        )
    update = jnp.concatenate(rows, axis=0)
    return (update, new_momentum)


def solution(mesh):
    in_specs = (P("dp", "tensor", None), P("dp", "tensor", None), P())
    out_specs = (P(None, "tensor", None), P("dp", "tensor", None))
    return jax.shard_map(
        per_device, mesh=mesh, in_specs=in_specs, out_specs=out_specs, check_vma=False
    )
```

```python
import math

import jax
import jax.numpy as jnp
from jax import lax
from jax.sharding import PartitionSpec as P

M = 576
N = 6144
ITERS = 2


coef_a = 3.4445
coef_b = -4.775
coef_c = 2.0315
decay = 0.95
eps = 1e-07


def _shift_pairs(size, s):
    return [(i, (i + s) % size) for i in range(size)]


def total_over(value, axis, size):
    spread = jnp.broadcast_to(value, (size, 1))
    got = lax.all_to_all(spread, axis, split_axis=0, concat_axis=0, tiled=True)
    return jnp.sum(got)


def gram_allreduce(partial, axis, size):
    n = partial.shape[0]
    h = n // 2
    upper_a = partial[:h, :h]
    block_b = partial[:h, h:]
    lower_c = partial[h:, h:]
    row = lax.broadcasted_iota(jnp.int32, (h, h), 0)
    col = lax.broadcasted_iota(jnp.int32, (h, h), 1)
    folded = jnp.where(row <= col, upper_a, lower_c)
    diag_c = jnp.sum(jnp.where(row == col, lower_c, 0.0), axis=0)
    payload = jnp.concatenate([folded, block_b], axis=1)
    extra = jnp.concatenate([diag_c, jnp.zeros((h,), jnp.float32)])[None, :]
    rows = -(-(h + 1) // size) * size
    payload = jnp.concatenate(
        [payload, extra, jnp.zeros((rows - h - 1, 2 * h), jnp.float32)], axis=0
    )
    per = rows // size
    blocks = payload.reshape(size, per, 2 * h)
    me = lax.axis_index(axis)
    acc = lax.dynamic_index_in_dim(blocks, me, 0, keepdims=False)
    for s in range(1, size):
        if size & (size - 1) == 0:
            target, pairs = me ^ s, [(i, i ^ s) for i in range(size)]
        else:
            target, pairs = (me + s) % size, _shift_pairs(size, s)
        outgoing = lax.dynamic_index_in_dim(blocks, target, 0, keepdims=False)
        acc = acc + lax.ppermute(outgoing, axis, pairs)
    mine = acc.astype(jnp.bfloat16)
    if size & (size - 1) == 0:
        count = per * 2 * h
        dense = -(-count // 2048) * 2048
        packed = jnp.pad(mine.reshape(count), (0, dense - count)).reshape(dense // 128, 128)
        relative = jnp.stack(
            [packed] + [lax.ppermute(packed, axis, [(i, i ^ k) for i in range(size)]) for k in range(1, size)]
        )
        order = jnp.arange(size, dtype=jnp.int32) ^ me
        ordered = jnp.take(relative, order, axis=0, mode="clip").reshape(size, dense)
        full = ordered[:, :count].reshape(rows, 2 * h)
    else:
        spread = jnp.broadcast_to(mine[None], (size,) + mine.shape)
        full = lax.all_to_all(spread, axis, split_axis=0, concat_axis=0, tiled=True).reshape(rows, 2 * h)
    folded_r = full[:h, :h]
    block_br = full[:h, h:]
    diag_cr = full[h, :h]
    upper_r = jnp.where(row <= col, folded_r, folded_r.T)
    lower_r = jnp.where(row > col, folded_r, folded_r.T)
    lower_r = jnp.where(row == col, diag_cr[None, :], lower_r)
    top = jnp.concatenate([upper_r, block_br], axis=1)
    bottom = jnp.concatenate([block_br.T, lower_r], axis=1)
    return jnp.concatenate([top, bottom], axis=0)


def gather_slots(mine, axis, size):
    if size & (size - 1) != 0:
        full = lax.all_gather(mine[None], axis, axis=0, tiled=True)
        me = lax.axis_index(axis)
        return jnp.take(full, jnp.arange(size, dtype=jnp.int32) ^ me, axis=0, mode="clip")
    held = {0: mine}
    bit = size // 2
    while bit >= 1:
        keys = sorted(held)
        sent = jnp.stack([held[j] for j in keys])
        got = lax.ppermute(sent, axis, [(i, i ^ bit) for i in range(size)])
        for n, j in enumerate(keys):
            held[j ^ bit] = got[n]
        bit //= 2
    return jnp.stack([held[j] for j in range(size)])


def per_device(grad, momentum, owner):
    size = lax.axis_size("tensor")
    new_momentum = decay * momentum + grad.astype(jnp.float32)
    direction = grad.astype(jnp.float32) + decay * new_momentum
    total = total_over(jnp.sum(direction * direction), "tensor", size)
    rows_here = (direction[0] / (jnp.sqrt(total) + eps)).astype(jnp.bfloat16)
    if size & (size - 1) == 0:
        me = lax.axis_index("tensor")
        width = rows_here.shape[1] // size
        by_col = rows_here.reshape(rows_here.shape[0], size, width)
        got = [lax.dynamic_index_in_dim(by_col, me, 1, keepdims=False)]
        for k in range(1, size):
            outgoing = lax.dynamic_index_in_dim(by_col, me ^ k, 1, keepdims=False)
            got.append(lax.ppermute(outgoing, "tensor", [(i, i ^ k) for i in range(size)]))
        relative = jnp.stack(got)
        order = jnp.arange(size, dtype=jnp.int32) ^ me
        columns = jnp.take(relative, order, axis=0, mode="clip").reshape(size * rows_here.shape[0], width)
    else:
        columns = lax.all_to_all(rows_here, "tensor", split_axis=1, concat_axis=0, tiled=True)
    for step in range(ITERS):
        partial = jnp.dot(columns, columns.T, preferred_element_type=jnp.float32)
        gram = gram_allreduce(partial, "tensor", size)
        square = jnp.dot(gram, gram, preferred_element_type=jnp.float32)
        poly = (coef_b * gram.astype(jnp.float32) + coef_c * square).astype(jnp.bfloat16)
        applied = jnp.dot(poly, columns, preferred_element_type=jnp.float32)
        columns = (coef_a * columns.astype(jnp.float32) + applied).astype(jnp.bfloat16)
    factor = 0.2 * math.sqrt(max(M, N))
    per = columns.shape[0] // size
    half = min(per, 8 * ((per * 9 + 64) // 128))
    blocks = columns.reshape(size, per, columns.shape[1])
    slots = lax.axis_size("dp")
    ids = jnp.arange(slots, dtype=jnp.int32)
    inverse = jnp.sum(
        jnp.where(owner[None, :] == ids[:, None], ids[None, :], 0), axis=1
    )
    where_from = inverse ^ lax.axis_index("dp")
    bounds = ((0, half), (half, per)) if half < per else ((0, per),)
    parts = [
        blocks[:, lo:hi, :].reshape(size * (hi - lo), columns.shape[1]) for lo, hi in bounds
    ]
    pieces = []
    for n in range(len(parts)):
        back_rows = lax.all_to_all(parts[n], "tensor", split_axis=0, concat_axis=1, tiled=True)
        if n + 1 < len(parts):
            parts[n + 1], back_rows = lax.optimization_barrier((parts[n + 1], back_rows))
        scaled = (factor * back_rows.astype(jnp.float32)).astype(jnp.bfloat16)
        pieces.append(gather_slots(scaled, "dp", slots))
    rows = []
    for m in range(slots):
        rows.append(
            jnp.concatenate(
                [lax.dynamic_index_in_dim(p, where_from[m], 0, keepdims=True) for p in pieces],
                axis=1,
            )
        )
    update = jnp.concatenate(rows, axis=0)
    return (update, new_momentum)


def solution(mesh):
    in_specs = (P("dp", "tensor", None), P("dp", "tensor", None), P())
    out_specs = (P(None, "tensor", None), P("dp", "tensor", None))
    return jax.shard_map(
        per_device, mesh=mesh, in_specs=in_specs, out_specs=out_specs, check_vma=False
    )
```

```python
import math

import jax
import jax.numpy as jnp
from jax import lax
from jax.sharding import PartitionSpec as P

M = 576
N = 6144
ITERS = 2


coef_a = 3.4445
coef_b = -4.775
coef_c = 2.0315
decay = 0.95
eps = 1e-07


def _shift_pairs(size, s):
    return [(i, (i + s) % size) for i in range(size)]


def total_over(value, axis, size):
    spread = jnp.broadcast_to(value, (size, 1))
    got = lax.all_to_all(spread, axis, split_axis=0, concat_axis=0, tiled=True)
    return jnp.sum(got)


def gram_allreduce(partial, axis, size):
    n = partial.shape[0]
    h = n // 2
    upper_a = partial[:h, :h]
    block_b = partial[:h, h:]
    lower_c = partial[h:, h:]
    row = lax.broadcasted_iota(jnp.int32, (h, h), 0)
    col = lax.broadcasted_iota(jnp.int32, (h, h), 1)
    folded = jnp.where(row <= col, upper_a, lower_c)
    diag_c = jnp.sum(jnp.where(row == col, lower_c, 0.0), axis=0)
    payload = jnp.concatenate([folded, block_b], axis=1)
    extra = jnp.concatenate([diag_c, jnp.zeros((h,), jnp.float32)])[None, :]
    rows = -(-(h + 1) // size) * size
    payload = jnp.concatenate(
        [payload, extra, jnp.zeros((rows - h - 1, 2 * h), jnp.float32)], axis=0
    )
    per = rows // size
    blocks = payload.reshape(size, per, 2 * h)
    me = lax.axis_index(axis)
    acc = lax.dynamic_index_in_dim(blocks, me, 0, keepdims=False)
    for s in range(1, size):
        if size & (size - 1) == 0:
            target, pairs = me ^ s, [(i, i ^ s) for i in range(size)]
        else:
            target, pairs = (me + s) % size, _shift_pairs(size, s)
        outgoing = lax.dynamic_index_in_dim(blocks, target, 0, keepdims=False)
        acc = acc + lax.ppermute(outgoing, axis, pairs)
    mine = acc.astype(jnp.bfloat16)
    if size & (size - 1) == 0:
        count = per * 2 * h
        dense = -(-count // 2048) * 2048
        packed = jnp.pad(mine.reshape(count), (0, dense - count)).reshape(dense // 128, 128)
        relative = jnp.stack(
            [packed] + [lax.ppermute(packed, axis, [(i, i ^ k) for i in range(size)]) for k in range(1, size)]
        )
        order = jnp.arange(size, dtype=jnp.int32) ^ me
        ordered = jnp.take(relative, order, axis=0, mode="clip").reshape(size, dense)
        full = ordered[:, :count].reshape(rows, 2 * h)
    else:
        spread = jnp.broadcast_to(mine[None], (size,) + mine.shape)
        full = lax.all_to_all(spread, axis, split_axis=0, concat_axis=0, tiled=True).reshape(rows, 2 * h)
    folded_r = full[:h, :h]
    block_br = full[:h, h:]
    diag_cr = full[h, :h]
    upper_r = jnp.where(row <= col, folded_r, folded_r.T)
    lower_r = jnp.where(row > col, folded_r, folded_r.T)
    lower_r = jnp.where(row == col, diag_cr[None, :], lower_r)
    top = jnp.concatenate([upper_r, block_br], axis=1)
    bottom = jnp.concatenate([block_br.T, lower_r], axis=1)
    return jnp.concatenate([top, bottom], axis=0)


def gather_slots(mine, axis, size):
    if size & (size - 1) != 0:
        full = lax.all_gather(mine[None], axis, axis=0, tiled=True)
        me = lax.axis_index(axis)
        return jnp.take(full, jnp.arange(size, dtype=jnp.int32) ^ me, axis=0, mode="clip")
    held = {0: mine}
    bit = size // 2
    while bit >= 1:
        keys = sorted(held)
        sent = jnp.stack([held[j] for j in keys])
        got = lax.ppermute(sent, axis, [(i, i ^ bit) for i in range(size)])
        for n, j in enumerate(keys):
            held[j ^ bit] = got[n]
        bit //= 2
    return jnp.stack([held[j] for j in range(size)])


def per_device(grad, momentum, owner):
    size = lax.axis_size("tensor")
    new_momentum = decay * momentum + grad.astype(jnp.float32)
    direction = grad.astype(jnp.float32) + decay * new_momentum
    total = total_over(jnp.sum(direction * direction), "tensor", size)
    rows_here = (direction[0] / (jnp.sqrt(total) + eps)).astype(jnp.bfloat16)
    if size & (size - 1) == 0:
        me = lax.axis_index("tensor")
        width = rows_here.shape[1] // size
        by_col = rows_here.reshape(rows_here.shape[0], size, width)
        count = rows_here.shape[0] * width
        dense = -(-count // 2048) * 2048

        def packed(k):
            block = lax.dynamic_index_in_dim(by_col, me ^ k, 1, keepdims=False).reshape(count)
            return jnp.pad(block, (0, dense - count)).reshape(dense // 128, 128)

        got = [packed(0)]
        for k in range(1, size):
            got.append(lax.ppermute(packed(k), "tensor", [(i, i ^ k) for i in range(size)]))
        relative = jnp.stack(got).reshape(size, dense)[:, :count]
        relative = relative.reshape(size, rows_here.shape[0], width)
        order = jnp.arange(size, dtype=jnp.int32) ^ me
        columns = jnp.take(relative, order, axis=0, mode="clip").reshape(size * rows_here.shape[0], width)
    else:
        columns = lax.all_to_all(rows_here, "tensor", split_axis=1, concat_axis=0, tiled=True)
    for step in range(ITERS):
        partial = jnp.dot(columns, columns.T, preferred_element_type=jnp.float32)
        gram = gram_allreduce(partial, "tensor", size)
        square = jnp.dot(gram, gram, preferred_element_type=jnp.float32)
        poly = (coef_b * gram.astype(jnp.float32) + coef_c * square).astype(jnp.bfloat16)
        applied = jnp.dot(poly, columns, preferred_element_type=jnp.float32)
        columns = (coef_a * columns.astype(jnp.float32) + applied).astype(jnp.bfloat16)
    factor = 0.2 * math.sqrt(max(M, N))
    per = columns.shape[0] // size
    half = min(per, 8 * ((per * 9 + 64) // 128))
    blocks = columns.reshape(size, per, columns.shape[1])
    slots = lax.axis_size("dp")
    ids = jnp.arange(slots, dtype=jnp.int32)
    inverse = jnp.sum(
        jnp.where(owner[None, :] == ids[:, None], ids[None, :], 0), axis=1
    )
    where_from = inverse ^ lax.axis_index("dp")
    bounds = ((0, half), (half, per)) if half < per else ((0, per),)
    parts = [
        blocks[:, lo:hi, :].reshape(size * (hi - lo), columns.shape[1]) for lo, hi in bounds
    ]
    pieces = []
    for n in range(len(parts)):
        back_rows = lax.all_to_all(parts[n], "tensor", split_axis=0, concat_axis=1, tiled=True)
        if n + 1 < len(parts):
            parts[n + 1], back_rows = lax.optimization_barrier((parts[n + 1], back_rows))
        scaled = (factor * back_rows.astype(jnp.float32)).astype(jnp.bfloat16)
        pieces.append(gather_slots(scaled, "dp", slots))
    rows = []
    for m in range(slots):
        rows.append(
            jnp.concatenate(
                [lax.dynamic_index_in_dim(p, where_from[m], 0, keepdims=True) for p in pieces],
                axis=1,
            )
        )
    update = jnp.concatenate(rows, axis=0)
    return (update, new_momentum)


def solution(mesh):
    in_specs = (P("dp", "tensor", None), P("dp", "tensor", None), P())
    out_specs = (P(None, "tensor", None), P("dp", "tensor", None))
    return jax.shard_map(
        per_device, mesh=mesh, in_specs=in_specs, out_specs=out_specs, check_vma=False
    )
```

```python
import math

import jax
import jax.numpy as jnp
from jax import lax
from jax.sharding import PartitionSpec as P

M = 576
N = 6144
ITERS = 2


coef_a = 3.4445
coef_b = -4.775
coef_c = 2.0315
decay = 0.95
eps = 1e-07


def _shift_pairs(size, s):
    return [(i, (i + s) % size) for i in range(size)]


def total_over(value, axis, size):
    spread = jnp.broadcast_to(value, (size, 1))
    got = lax.all_to_all(spread, axis, split_axis=0, concat_axis=0, tiled=True)
    return jnp.sum(got)


def gram_allreduce(partial, axis, size):
    n = partial.shape[0]
    h = n // 2
    upper_a = partial[:h, :h]
    block_b = partial[:h, h:]
    lower_c = partial[h:, h:]
    row = lax.broadcasted_iota(jnp.int32, (h, h), 0)
    col = lax.broadcasted_iota(jnp.int32, (h, h), 1)
    folded = jnp.where(row <= col, upper_a, lower_c)
    diag_c = jnp.sum(jnp.where(row == col, lower_c, 0.0), axis=0)
    payload = jnp.concatenate([folded, block_b], axis=1)
    extra = jnp.concatenate([diag_c, jnp.zeros((h,), jnp.float32)])[None, :]
    rows = -(-(h + 1) // size) * size
    payload = jnp.concatenate(
        [payload, extra, jnp.zeros((rows - h - 1, 2 * h), jnp.float32)], axis=0
    )
    per = rows // size
    blocks = payload.reshape(size, per, 2 * h)
    me = lax.axis_index(axis)
    if size & (size - 1) == 0:
        count = per * 2 * h
        dense = -(-count // 2048) * 2048
        blocks = jnp.pad(blocks.reshape(size, count), ((0, 0), (0, dense - count)))
        blocks = blocks.reshape(size, dense // 128, 128)
    acc = lax.dynamic_index_in_dim(blocks, me, 0, keepdims=False)
    for s in range(1, size):
        if size & (size - 1) == 0:
            target, pairs = me ^ s, [(i, i ^ s) for i in range(size)]
        else:
            target, pairs = (me + s) % size, _shift_pairs(size, s)
        outgoing = lax.dynamic_index_in_dim(blocks, target, 0, keepdims=False)
        acc = acc + lax.ppermute(outgoing, axis, pairs)
    mine = acc.astype(jnp.bfloat16)
    if size & (size - 1) == 0:
        relative = jnp.stack(
            [mine] + [lax.ppermute(mine, axis, [(i, i ^ k) for i in range(size)]) for k in range(1, size)]
        )
        order = jnp.arange(size, dtype=jnp.int32) ^ me
        ordered = jnp.take(relative, order, axis=0, mode="clip").reshape(size, dense)
        full = ordered[:, :count].reshape(rows, 2 * h)
    else:
        spread = jnp.broadcast_to(mine[None], (size,) + mine.shape)
        full = lax.all_to_all(spread, axis, split_axis=0, concat_axis=0, tiled=True).reshape(rows, 2 * h)
    folded_r = full[:h, :h]
    block_br = full[:h, h:]
    diag_cr = full[h, :h]
    upper_r = jnp.where(row <= col, folded_r, folded_r.T)
    lower_r = jnp.where(row > col, folded_r, folded_r.T)
    lower_r = jnp.where(row == col, diag_cr[None, :], lower_r)
    top = jnp.concatenate([upper_r, block_br], axis=1)
    bottom = jnp.concatenate([block_br.T, lower_r], axis=1)
    return jnp.concatenate([top, bottom], axis=0)


def gather_slots(mine, axis, size):
    if size & (size - 1) != 0:
        full = lax.all_gather(mine[None], axis, axis=0, tiled=True)
        me = lax.axis_index(axis)
        return jnp.take(full, jnp.arange(size, dtype=jnp.int32) ^ me, axis=0, mode="clip")
    held = {0: mine}
    bit = size // 2
    while bit >= 1:
        keys = sorted(held)
        sent = jnp.stack([held[j] for j in keys])
        got = lax.ppermute(sent, axis, [(i, i ^ bit) for i in range(size)])
        for n, j in enumerate(keys):
            held[j ^ bit] = got[n]
        bit //= 2
    return jnp.stack([held[j] for j in range(size)])


def per_device(grad, momentum, owner):
    size = lax.axis_size("tensor")
    new_momentum = decay * momentum + grad.astype(jnp.float32)
    direction = grad.astype(jnp.float32) + decay * new_momentum
    total = total_over(jnp.sum(direction * direction), "tensor", size)
    rows_here = (direction[0] / (jnp.sqrt(total) + eps)).astype(jnp.bfloat16)
    if size & (size - 1) == 0:
        me = lax.axis_index("tensor")
        width = rows_here.shape[1] // size
        by_col = rows_here.reshape(rows_here.shape[0], size, width)
        got = [lax.dynamic_index_in_dim(by_col, me, 1, keepdims=False)]
        for k in range(1, size):
            outgoing = lax.dynamic_index_in_dim(by_col, me ^ k, 1, keepdims=False)
            got.append(lax.ppermute(outgoing, "tensor", [(i, i ^ k) for i in range(size)]))
        relative = jnp.stack(got)
        order = jnp.arange(size, dtype=jnp.int32) ^ me
        columns = jnp.take(relative, order, axis=0, mode="clip").reshape(size * rows_here.shape[0], width)
    else:
        columns = lax.all_to_all(rows_here, "tensor", split_axis=1, concat_axis=0, tiled=True)
    for step in range(ITERS):
        partial = jnp.dot(columns, columns.T, preferred_element_type=jnp.float32)
        gram = gram_allreduce(partial, "tensor", size)
        square = jnp.dot(gram, gram, preferred_element_type=jnp.float32)
        poly = (coef_b * gram.astype(jnp.float32) + coef_c * square).astype(jnp.bfloat16)
        applied = jnp.dot(poly, columns, preferred_element_type=jnp.float32)
        columns = (coef_a * columns.astype(jnp.float32) + applied).astype(jnp.bfloat16)
    factor = 0.2 * math.sqrt(max(M, N))
    per = columns.shape[0] // size
    half = min(per, 8 * ((per * 9 + 64) // 128))
    blocks = columns.reshape(size, per, columns.shape[1])
    slots = lax.axis_size("dp")
    ids = jnp.arange(slots, dtype=jnp.int32)
    inverse = jnp.sum(
        jnp.where(owner[None, :] == ids[:, None], ids[None, :], 0), axis=1
    )
    where_from = inverse ^ lax.axis_index("dp")
    bounds = ((0, half), (half, per)) if half < per else ((0, per),)
    parts = [
        blocks[:, lo:hi, :].reshape(size * (hi - lo), columns.shape[1]) for lo, hi in bounds
    ]
    pieces = []
    for n in range(len(parts)):
        back_rows = lax.all_to_all(parts[n], "tensor", split_axis=0, concat_axis=1, tiled=True)
        if n + 1 < len(parts):
            parts[n + 1], back_rows = lax.optimization_barrier((parts[n + 1], back_rows))
        scaled = (factor * back_rows.astype(jnp.float32)).astype(jnp.bfloat16)
        pieces.append(gather_slots(scaled, "dp", slots))
    rows = []
    for m in range(slots):
        rows.append(
            jnp.concatenate(
                [lax.dynamic_index_in_dim(p, where_from[m], 0, keepdims=True) for p in pieces],
                axis=1,
            )
        )
    update = jnp.concatenate(rows, axis=0)
    return (update, new_momentum)


def solution(mesh):
    in_specs = (P("dp", "tensor", None), P("dp", "tensor", None), P())
    out_specs = (P(None, "tensor", None), P("dp", "tensor", None))
    return jax.shard_map(
        per_device, mesh=mesh, in_specs=in_specs, out_specs=out_specs, check_vma=False
    )
```
